32 devices in a mesh: dp: 4 (over x, core), seq: 8 (over z, y).
Axes of the slice: x: 2, y: 2, z: 4, core: 2. Of those that a mesh axis runs over, the one named last changes fastest.
Arguments:
- queries: bfloat16 [4, 4096, 2048], P('dp', 'seq'), may hold values from -34 to 34
- neighbour_input: bfloat16 [4, 32, 64, 896], P('dp', 'seq'), may hold values from -6 to 6
- owner_list: int32 [4, 64, 2], P('dp', 'seq'), may hold values from 0 to 7, as said below
- block_list: int32 [4, 64, 2], P('dp', 'seq'), may hold values from 0 to 3
- enc_gain: float32 [896], replicated, may hold values from 0.5 to 8
- enc_attn: bfloat16 [4, 896, 896], P(None, 'dp'), may hold values from -0.1875 to 0.1875
- kv_weight: bfloat16 [2, 896, 2048], replicated, may hold values from -0.1875 to 0.1875
Outputs:
- context: bfloat16 [4, 4096, 2048], P('dp', 'seq')
The draws below stay inside these ranges and needn't reach their ends.
Inputs may be any that keep to these rules, and one draw needn't show every extreme that they name: `owner_list`: within the spans of one device, no owner is named more than 2 times; every owner is named in every sequence.
All inputs are finite; a program needn't handle non-finite values.
Results may differ from the reference program's by a relative error of at most 0.025.
The reference program's roundings to bfloat16 on the way count: a program that leaves them out, or rounds other values in their place, can miss the bound.
Values may be sent and summed in bfloat16 or wider, within the bound.
No kernel may reach another device: no remote copies, remote signals or barrier semaphores. Data moves between devices by JAX's collectives and lax.ppermute only.
A program may use at most 128 MiB of HBM per device.

```python
import jax
import jax.numpy as jnp
from jax import lax

HEADS = 16
HEAD_DIM = 128
ENC = 896
ENC_HEADS = 7
NLEN = 64
SPAN = 64
NEIGH = 2
NB_DEV = 4
QW = 2048
REQ = 16
ROWS = 4
LENGTH = 4096
SPANS = 64
BLOCKS = 32
N_SEQ = 8


def draw_owner_list(key, part):
    first, second = jax.random.split(key)
    owner_ids = jnp.arange(N_SEQ, dtype=jnp.int32)
    popular = jax.random.randint(first, (ROWS, 1, N_SEQ), 0, 4) * 1048576
    noise = jax.random.randint(second, (ROWS, N_SEQ, N_SEQ), 0, 1048576)
    forced = ((owner_ids[:, None] + 1) % N_SEQ == owner_ids[None, :]).astype(jnp.int32) * 268435456
    scores = (popular + noise) * N_SEQ + owner_ids[None, None, :] + forced[None, :, :]
    ranked = lax.top_k(scores, N_SEQ)[1]
    picks = ranked[:, :, jnp.arange(REQ) % N_SEQ]
    return picks.reshape(ROWS, SPANS, NEIGH).astype(jnp.int32)


def draw_queries(key, part):
    first = jax.random.fold_in(key, 0)
    values = jnp.clip(jax.random.normal(first, (ROWS, LENGTH, QW), jnp.float32), -6.0, 6.0)
    return values.astype(jnp.bfloat16)


def draw_enc_gain(key, part):
    values = jax.random.uniform(key, (ENC,), jnp.float32, 0.5, 1.5)
    return values


def set_ends(entries, own_key, least, high):
    shape = entries.shape
    place = [jax.random.randint(jax.random.fold_in(own_key, axis), (), 0, shape[axis]) for axis in range(len(shape))]
    entries = entries.at[tuple(place)].set(least)
    longest = shape.index(max(shape))
    place[longest] = (place[longest] + 1) % shape[longest]
    return entries.at[tuple(place)].set(high)


def block_scale(own_key, shape, pieces, least, top_value):
    factor_of, own = 1.0, jax.random.fold_in(own_key, 6)
    for dim, parts in pieces:
        heights = jnp.exp(jax.random.uniform(jax.random.fold_in(own, dim), (parts,), jnp.float32, least / len(pieces), top_value / len(pieces)))
        factor_of = factor_of * jnp.repeat(heights, shape[dim] // parts).reshape([-1 if axis == dim else 1 for axis in range(len(shape))])
    return factor_of


def normal_values(own_key, shape, scale, most, cuts=(), kind=jnp.bfloat16):
    drawn = jax.random.normal(own_key, shape, jnp.float32) * scale
    if len(cuts) > 0:
        drawn = block_scale(own_key, shape, cuts, -0.22, 0.18) * drawn
    return jnp.clip(drawn, min=-most, max=most).astype(kind)


def setup_inputs(seed: int = 0) -> dict:
    key_list = jax.random.split(jax.random.key(seed), 8)
    queries = draw_queries(jax.random.fold_in(key_list[7], 71), 0)
    neighbour_input = normal_values(key_list[1], (ROWS, BLOCKS, NLEN, ENC), 1.0, 6.0, ((0, 4), (1, 8)))
    owner_list = draw_owner_list(jax.random.fold_in(key_list[7], 71), 0)
    block_list = set_ends(jax.random.randint(key_list[3], (ROWS, SPANS, NEIGH), 0, NB_DEV), jax.random.fold_in(key_list[3], 1), 0, NB_DEV - 1).astype(jnp.int32)
    enc_gain = draw_enc_gain(jax.random.fold_in(key_list[7], 71), 0)
    enc_attn = normal_values(key_list[5], (4, ENC, ENC), ENC ** -0.5, 0.1875, ((1, 4),))
    kv_weight = normal_values(key_list[6], (2, ENC, QW), ENC ** -0.5, 0.1875)
    return {"queries": queries, "neighbour_input": neighbour_input, "owner_list": owner_list, "block_list": block_list, "enc_gain": enc_gain, "enc_attn": enc_attn, "kv_weight": kv_weight}


epsilon = 1e-05

def softmax_rows(scores):
    highest = lax.optimization_barrier(jnp.max(scores, axis=-1, keepdims=True))
    raised = jnp.exp(scores - highest)
    return raised / lax.optimization_barrier(jnp.sum(raised, axis=-1, keepdims=True))

def encode(blocks, gain, attention):
    inputs = blocks.astype(jnp.float32)
    spread = lax.optimization_barrier(jnp.mean(inputs * inputs, axis=-1, keepdims=True))
    normed = (inputs * lax.rsqrt(spread + epsilon) * gain).astype(jnp.bfloat16)
    count, length, width = blocks.shape
    head_size = width // ENC_HEADS
    projected = jnp.einsum('nte,pef->pntf', normed.astype(jnp.float32), attention[:3].astype(jnp.float32)).astype(jnp.bfloat16)
    split_heads = projected.reshape(3, count, length, ENC_HEADS, head_size)
    scores = jnp.einsum('nqhd,nkhd->nhqk', split_heads[0].astype(jnp.float32), split_heads[1].astype(jnp.float32)) * head_size ** (-0.5)
    weights = softmax_rows(scores).astype(jnp.bfloat16)
    mixture = jnp.einsum('nhqk,nkhd->nqhd', weights.astype(jnp.float32), split_heads[2].astype(jnp.float32)).astype(jnp.bfloat16)
    mixture = mixture.reshape(count, length, width)
    output = jnp.einsum('nte,ef->ntf', mixture.astype(jnp.float32), attention[3].astype(jnp.float32))
    return (inputs + output).astype(jnp.bfloat16)

def reference(queries, neighbour_input, owner_list, block_list, enc_gain, enc_attn, kv_weight):

    def one_row(row):
        row_queries, row_blocks, row_owners, row_index = row
        encoded = encode(row_blocks, enc_gain, enc_attn)
        key_value = jnp.einsum('bte,pef->pbtf', encoded.astype(jnp.float32), kv_weight.astype(jnp.float32)).astype(jnp.bfloat16)
        global_ids = (row_owners * NB_DEV + row_index).reshape(-1).astype(jnp.int32)
        chosen = jnp.take(key_value, global_ids, axis=1)
        span_count = row_queries.shape[0] // SPAN
        keys = chosen[0].reshape(span_count, NEIGH * NLEN, HEADS, HEAD_DIM)
        values = chosen[1].reshape(span_count, NEIGH * NLEN, HEADS, HEAD_DIM)
        grouped = row_queries.reshape(span_count, SPAN, HEADS, HEAD_DIM)
        scores = jnp.einsum('cqhd,ckhd->chqk', grouped.astype(jnp.float32), keys.astype(jnp.float32)) * HEAD_DIM ** (-0.5)
        weights = softmax_rows(scores).astype(jnp.bfloat16)
        mixture = jnp.einsum('chqk,ckhd->cqhd', weights.astype(jnp.float32), values.astype(jnp.float32)).astype(jnp.bfloat16)
        return mixture.reshape(row_queries.shape)
    return lax.map(one_row, (queries, neighbour_input, owner_list, block_list))
```

```python
import jax
import jax.numpy as jnp
from jax import lax
from jax.sharding import PartitionSpec as P

HEADS = 16
HEAD_DIM = 128
ENC_HEADS = 7
NLEN = 64
SPAN = 64
NEIGH = 2
NB_DEV = 4


epsilon = 1e-05


def softmax_rows(scores):
    highest = jnp.max(scores, axis=-1, keepdims=True)
    raised = jnp.exp(scores - highest)
    return raised / jnp.sum(raised, axis=-1, keepdims=True)


def encode(blocks, gain, attention):
    inputs = blocks.astype(jnp.float32)
    spread = jnp.mean(inputs * inputs, axis=-1, keepdims=True)
    normed = (inputs * lax.rsqrt(spread + epsilon) * gain).astype(jnp.bfloat16)
    count, length, width = blocks.shape
    head_size = width // ENC_HEADS
    projected = jnp.einsum(
        "nte,pef->pntf", normed, attention[:3], preferred_element_type=jnp.float32
    ).astype(jnp.bfloat16)
    split_heads = projected.reshape(3, count, length, ENC_HEADS, head_size)
    scores = jnp.einsum(
        "nqhd,nkhd->nhqk", split_heads[0], split_heads[1], preferred_element_type=jnp.float32
    ) * head_size ** (-0.5)
    weights = softmax_rows(scores).astype(jnp.bfloat16)
    mixture = jnp.einsum(
        "nhqk,nkhd->nqhd", weights, split_heads[2], preferred_element_type=jnp.float32
    ).astype(jnp.bfloat16)
    mixture = mixture.reshape(count, length, width)
    output = jnp.einsum("nte,ef->ntf", mixture, attention[3], preferred_element_type=jnp.float32)
    return (inputs + output).astype(jnp.bfloat16)


def make_shards(n_seq):
    def shards(queries, neighbour_input, owner_list, block_list, enc_gain, enc_attn, kv_weight):
        full_weights = lax.all_gather(enc_attn, "dp", axis=1, tiled=True)
        me = lax.axis_index("seq")
        owners = owner_list.reshape(-1)
        indices = block_list.reshape(-1)
        refs = owners.shape[0]
        per_owner = -(-refs // n_seq)
        same = owners[:, None] == owners[None, :]
        earlier = jnp.arange(refs)[None, :] < jnp.arange(refs)[:, None]
        rank = jnp.sum(same & earlier, axis=1).astype(jnp.int32)
        asks = jnp.stack([owners, indices, rank])
        asks = jnp.broadcast_to(asks[None], (n_seq, 3, refs))
        asked = lax.all_to_all(asks, "seq", 0, 0, tiled=True)
        slots = jnp.arange(per_owner, dtype=jnp.int32)
        match = (asked[:, 0, None, :] == me) & (asked[:, 2, None, :] == slots[None, :, None])
        picks = jnp.sum(jnp.where(match, asked[:, 1, None, :], 0), axis=-1)
        sent = jnp.take(neighbour_input[0], picks.reshape(-1), axis=0, mode="clip")
        sent = sent.reshape(n_seq, per_owner, NLEN, neighbour_input.shape[-1])
        got = lax.all_to_all(sent, "seq", 0, 0, tiled=True)
        got = got.reshape(n_seq * per_owner, NLEN, neighbour_input.shape[-1])
        chosen_raw = jnp.take(got, owners * per_owner + rank, axis=0, mode="clip")
        chosen = encode(chosen_raw, enc_gain, full_weights)
        key_value = jnp.einsum(
            "rte,pef->prtf", chosen, kv_weight, preferred_element_type=jnp.float32
        ).astype(jnp.bfloat16)
        span_count = queries.shape[1] // SPAN
        memory_keys = key_value[0].reshape(span_count, NEIGH * NLEN, HEADS, HEAD_DIM)
        memory_values = key_value[1].reshape(span_count, NEIGH * NLEN, HEADS, HEAD_DIM)
        grouped = queries[0].reshape(span_count, SPAN, HEADS, HEAD_DIM)
        scores = jnp.einsum(
            "cqhd,ckhd->chqk", grouped, memory_keys, preferred_element_type=jnp.float32
        ) * HEAD_DIM ** (-0.5)
        weights = softmax_rows(scores).astype(jnp.bfloat16)
        mixture = jnp.einsum(
            "chqk,ckhd->cqhd", weights, memory_values, preferred_element_type=jnp.float32
        ).astype(jnp.bfloat16)
        return mixture.reshape(queries.shape)

    return shards


def solution(mesh):
    return jax.shard_map(
        make_shards(mesh.shape["seq"]),
        mesh=mesh,
        in_specs=(
            P("dp", "seq", None),
            P("dp", "seq", None, None),
            P("dp", "seq", None),
            P("dp", "seq", None),
            P(),
            P(None, "dp", None),
            P(),
        ),
        out_specs=P("dp", "seq", None),
        check_vma=False,
    )
```

```python
import jax
import jax.numpy as jnp
from jax import lax
from jax.experimental import pallas as pl
from jax.experimental.pallas import tpu as pltpu
from jax.sharding import PartitionSpec as P

HEADS = 16
HEAD_DIM = 128
ENC_HEADS = 7
NLEN = 64
SPAN = 64
NEIGH = 2
NB_DEV = 4


epsilon = 1e-05


def _softmax_bf16(scores):
    highest = jnp.max(scores, axis=-1, keepdims=True)
    raised = jnp.exp(scores - highest)
    return (raised / jnp.sum(raised, axis=-1, keepdims=True)).astype(jnp.bfloat16)


def _dot_t(a, b):
    return lax.dot_general(a, b, (((1,), (1,)), ((), ())), preferred_element_type=jnp.float32)


def _encoder_kernel(x_ref, gain_ref, w_ref, out_ref, qkv_ref, mix_ref):
    inputs = x_ref[...].astype(jnp.float32)
    spread = jnp.mean(inputs * inputs, axis=-1, keepdims=True)
    normed = (inputs * lax.rsqrt(spread + epsilon) * gain_ref[...]).astype(jnp.bfloat16)
    for p in range(3):
        qkv_ref[p] = jnp.dot(normed, w_ref[p], preferred_element_type=jnp.float32).astype(jnp.bfloat16)
    width = inputs.shape[-1]
    head_size = width // ENC_HEADS
    scale = head_size ** (-0.5)
    for b in range(inputs.shape[0] // NLEN):
        rows = pl.ds(b * NLEN, NLEN)
        for h in range(ENC_HEADS):
            cols = pl.ds(h * head_size, head_size)
            scores = _dot_t(qkv_ref[0, rows, cols], qkv_ref[1, rows, cols]) * scale
            weights = _softmax_bf16(scores)
            mix_ref[rows, cols] = jnp.dot(
                weights, qkv_ref[2, rows, cols], preferred_element_type=jnp.float32
            ).astype(jnp.bfloat16)
    output = jnp.dot(mix_ref[...], w_ref[3], preferred_element_type=jnp.float32)
    out_ref[...] = (inputs + output).astype(jnp.bfloat16)


def encode_blocks(blocks, gain, attention, group=4):
    count, length, width = blocks.shape
    rows = group * length
    flat = blocks.reshape(count * length, width)
    out = pl.pallas_call(
        _encoder_kernel,
        out_shape=jax.ShapeDtypeStruct(flat.shape, jnp.bfloat16),
        grid=(count // group,),
        in_specs=[
            pl.BlockSpec((rows, width), lambda i: (i, 0)),
            pl.BlockSpec((1, width), lambda i: (0, 0)),
            pl.BlockSpec(attention.shape, lambda i: (0, 0, 0)),
        ],
        out_specs=pl.BlockSpec((rows, width), lambda i: (i, 0)),
        scratch_shapes=[
            pltpu.VMEM((3, rows, width), jnp.bfloat16),
            pltpu.VMEM((rows, width), jnp.bfloat16),
        ],
    )(flat, gain.reshape(1, width), attention)
    return out


def _cross_kernel(q_ref, k_ref, v_ref, out_ref):
    scale = HEAD_DIM ** (-0.5)
    for h in range(q_ref.shape[-1] // HEAD_DIM):
        cols = pl.ds(h * HEAD_DIM, HEAD_DIM)
        scores = _dot_t(q_ref[:, cols], k_ref[:, cols]) * scale
        weights = _softmax_bf16(scores)
        out_ref[:, cols] = jnp.dot(
            weights, v_ref[:, cols], preferred_element_type=jnp.float32
        ).astype(jnp.bfloat16)


def cross_attend(queries, keys, values):
    length, width = queries.shape
    memory = NEIGH * NLEN
    return pl.pallas_call(
        _cross_kernel,
        out_shape=jax.ShapeDtypeStruct(queries.shape, jnp.bfloat16),
        grid=(length // SPAN,),
        in_specs=[
            pl.BlockSpec((SPAN, width), lambda c: (c, 0)),
            pl.BlockSpec((memory, width), lambda c: (c, 0)),
            pl.BlockSpec((memory, width), lambda c: (c, 0)),
        ],
        out_specs=pl.BlockSpec((SPAN, width), lambda c: (c, 0)),
    )(queries, keys, values)


def make_shards(n_seq):
    def shards(queries, neighbour_input, owner_list, block_list, enc_gain, enc_attn, kv_weight):
        full_weights = lax.all_gather(enc_attn, "dp", axis=1, tiled=True)
        me = lax.axis_index("seq")
        owners = owner_list.reshape(-1)
        indices = block_list.reshape(-1)
        refs = owners.shape[0]
        per_owner = -(-refs // n_seq)
        same = owners[:, None] == owners[None, :]
        earlier = jnp.arange(refs)[None, :] < jnp.arange(refs)[:, None]
        rank = jnp.sum(same & earlier, axis=1).astype(jnp.int32)
        asks = jnp.stack([owners, indices, rank])
        asks = jnp.broadcast_to(asks[None], (n_seq, 3, refs))
        asked = lax.all_to_all(asks, "seq", 0, 0, tiled=True)
        slots = jnp.arange(per_owner, dtype=jnp.int32)
        match = (asked[:, 0, None, :] == me) & (asked[:, 2, None, :] == slots[None, :, None])
        picks = jnp.sum(jnp.where(match, asked[:, 1, None, :], 0), axis=-1)
        sent = jnp.take(neighbour_input[0], picks.reshape(-1), axis=0, mode="clip")
        sent = sent.reshape(n_seq, per_owner, NLEN, neighbour_input.shape[-1])
        got = lax.all_to_all(sent, "seq", 0, 0, tiled=True)
        got = got.reshape(n_seq * per_owner, NLEN, neighbour_input.shape[-1])
        chosen_raw = jnp.take(got, owners * per_owner + rank, axis=0, mode="clip")
        chosen = encode_blocks(chosen_raw, enc_gain, full_weights)
        keys = jnp.dot(chosen, kv_weight[0], preferred_element_type=jnp.float32).astype(jnp.bfloat16)
        values = jnp.dot(chosen, kv_weight[1], preferred_element_type=jnp.float32).astype(jnp.bfloat16)
        return cross_attend(queries[0], keys, values)[None]

    return shards


def solution(mesh):
    return jax.shard_map(
        make_shards(mesh.shape["seq"]),
        mesh=mesh,
        in_specs=(
            P("dp", "seq", None),
            P("dp", "seq", None, None),
            P("dp", "seq", None),
            P("dp", "seq", None),
            P(),
            P(None, "dp", None),
            P(),
        ),
        out_specs=P("dp", "seq", None),
        check_vma=False,
    )
```

```python
import jax
import jax.numpy as jnp
from jax import lax
from jax.experimental import pallas as pl
from jax.experimental.pallas import tpu as pltpu
from jax.sharding import PartitionSpec as P

HEADS = 16
HEAD_DIM = 128
ENC_HEADS = 7
NLEN = 64
SPAN = 64
NEIGH = 2
NB_DEV = 4


epsilon = 1e-05


def _softmax_bf16(scores):
    highest = jnp.max(scores, axis=-1, keepdims=True)
    raised = jnp.exp(scores - highest)
    return (raised * (1.0 / jnp.sum(raised, axis=-1, keepdims=True))).astype(jnp.bfloat16)


def _encoder_kernel(x_ref, gain_ref, w_ref, out_ref, q_ref, kt_ref, v_ref, mix_ref):
    inputs = x_ref[...].astype(jnp.float32)
    spread = jnp.mean(inputs * inputs, axis=-1, keepdims=True)
    normed = (inputs * lax.rsqrt(spread + epsilon) * gain_ref[...]).astype(jnp.bfloat16)
    q_ref[...] = jnp.dot(normed, w_ref[0], preferred_element_type=jnp.float32).astype(jnp.bfloat16)
    v_ref[...] = jnp.dot(normed, w_ref[2], preferred_element_type=jnp.float32).astype(jnp.bfloat16)
    kt_ref[...] = jnp.dot(normed, w_ref[1], preferred_element_type=jnp.float32).T.astype(jnp.bfloat16)
    width = inputs.shape[-1]
    head_size = width // ENC_HEADS
    scale = head_size ** (-0.5)
    pair = 2 * NLEN
    rows_of = lax.broadcasted_iota(jnp.int32, (pair, pair), 0) // NLEN
    cols_of = lax.broadcasted_iota(jnp.int32, (pair, pair), 1) // NLEN
    same = rows_of == cols_of
    for b in range(inputs.shape[0] // pair):
        rows = pl.ds(b * pair, pair)
        for h in range(ENC_HEADS):
            cols = pl.ds(h * head_size, head_size)
            scores = jnp.dot(q_ref[rows, cols], kt_ref[cols, rows], preferred_element_type=jnp.float32) * scale
            weights = _softmax_bf16(jnp.where(same, scores, -jnp.inf))
            mix_ref[rows, cols] = jnp.dot(
                weights, v_ref[rows, cols], preferred_element_type=jnp.float32
            ).astype(jnp.bfloat16)
    output = jnp.dot(mix_ref[...], w_ref[3], preferred_element_type=jnp.float32)
    out_ref[...] = (inputs + output).astype(jnp.bfloat16)


def encode_blocks(blocks, gain, attention, group=8):
    count, length, width = blocks.shape
    group = min(group, count)
    rows = group * length
    flat = blocks.reshape(count * length, width)
    return pl.pallas_call(
        _encoder_kernel,
        out_shape=jax.ShapeDtypeStruct(flat.shape, jnp.bfloat16),
        grid=(count // group,),
        in_specs=[
            pl.BlockSpec((rows, width), lambda i: (i, 0)),
            pl.BlockSpec((1, width), lambda i: (0, 0)),
            pl.BlockSpec(attention.shape, lambda i: (0, 0, 0)),
        ],
        out_specs=pl.BlockSpec((rows, width), lambda i: (i, 0)),
        scratch_shapes=[
            pltpu.VMEM((rows, width), jnp.bfloat16),
            pltpu.VMEM((width, rows), jnp.bfloat16),
            pltpu.VMEM((rows, width), jnp.bfloat16),
            pltpu.VMEM((rows, width), jnp.bfloat16),
        ],
    )(flat, gain.reshape(1, width), attention)


def _cross_kernel(q_ref, kt_ref, v_ref, out_ref):
    scale = HEAD_DIM ** (-0.5)
    memory = NEIGH * NLEN
    for s in range(q_ref.shape[0] // SPAN):
        rq = pl.ds(s * SPAN, SPAN)
        rk = pl.ds(s * memory, memory)
        for h in range(q_ref.shape[-1] // HEAD_DIM):
            cols = pl.ds(h * HEAD_DIM, HEAD_DIM)
            scores = jnp.dot(q_ref[rq, cols], kt_ref[cols, rk], preferred_element_type=jnp.float32) * scale
            weights = _softmax_bf16(scores)
            out_ref[rq, cols] = jnp.dot(
                weights, v_ref[rk, cols], preferred_element_type=jnp.float32
            ).astype(jnp.bfloat16)


def cross_attend(queries, keys_t, values, group=4):
    length, width = queries.shape
    memory = NEIGH * NLEN
    group = min(group, length // SPAN)
    return pl.pallas_call(
        _cross_kernel,
        out_shape=jax.ShapeDtypeStruct(queries.shape, jnp.bfloat16),
        grid=(length // (SPAN * group),),
        in_specs=[
            pl.BlockSpec((SPAN * group, width), lambda c: (c, 0)),
            pl.BlockSpec((width, memory * group), lambda c: (0, c)),
            pl.BlockSpec((memory * group, width), lambda c: (c, 0)),
        ],
        out_specs=pl.BlockSpec((SPAN * group, width), lambda c: (c, 0)),
    )(queries, keys_t, values)


def make_shards(n_seq):
    def shards(queries, neighbour_input, owner_list, block_list, enc_gain, enc_attn, kv_weight):
        full_weights = lax.all_gather(enc_attn, "dp", axis=1, tiled=True)
        me = lax.axis_index("seq")
        owners = owner_list.reshape(-1)
        indices = block_list.reshape(-1)
        refs = owners.shape[0]
        per_owner = -(-refs // n_seq)
        same = owners[:, None] == owners[None, :]
        earlier = jnp.arange(refs)[None, :] < jnp.arange(refs)[:, None]
        rank = jnp.sum(same & earlier, axis=1).astype(jnp.int32)
        asks = jnp.stack([owners, indices, rank])
        asks = jnp.broadcast_to(asks[None], (n_seq, 3, refs))
        asked = lax.all_to_all(asks, "seq", 0, 0, tiled=True)
        slots = jnp.arange(per_owner, dtype=jnp.int32)
        match = (asked[:, 0, None, :] == me) & (asked[:, 2, None, :] == slots[None, :, None])
        picks = jnp.sum(jnp.where(match, asked[:, 1, None, :], 0), axis=-1)
        sent = jnp.take(neighbour_input[0], picks.reshape(-1), axis=0, mode="clip")
        sent = sent.reshape(n_seq, per_owner, NLEN, neighbour_input.shape[-1])
        got = lax.all_to_all(sent, "seq", 0, 0, tiled=True)
        got = got.reshape(n_seq * per_owner, NLEN, neighbour_input.shape[-1])
        chosen_raw = jnp.take(got, owners * per_owner + rank, axis=0, mode="clip")
        chosen = encode_blocks(chosen_raw, enc_gain, full_weights)
        keys_t = jnp.einsum(
            "ef,re->fr", kv_weight[0], chosen, preferred_element_type=jnp.float32
        ).astype(jnp.bfloat16)
        values = jnp.dot(chosen, kv_weight[1], preferred_element_type=jnp.float32).astype(jnp.bfloat16)
        return cross_attend(queries[0], keys_t, values)[None]

    return shards


def solution(mesh):
    return jax.shard_map(
        make_shards(mesh.shape["seq"]),
        mesh=mesh,
        in_specs=(
            P("dp", "seq", None),
            P("dp", "seq", None, None),
            P("dp", "seq", None),
            P("dp", "seq", None),
            P(),
            P(None, "dp", None),
            P(),
        ),
        out_specs=P("dp", "seq", None),
        check_vma=False,
    )
```

```python
import jax
import jax.numpy as jnp
from jax import lax
from jax.experimental import pallas as pl
from jax.experimental.pallas import tpu as pltpu
from jax.sharding import PartitionSpec as P

HEADS = 16
HEAD_DIM = 128
ENC_HEADS = 7
NLEN = 64
SPAN = 64
NEIGH = 2
NB_DEV = 4


epsilon = 1e-05


def _softmax_bf16(scores):
    highest = jnp.max(scores, axis=-1, keepdims=True)
    raised = jnp.exp(scores - highest)
    return (raised * (1.0 / jnp.sum(raised, axis=-1, keepdims=True))).astype(jnp.bfloat16)


def _encoder_kernel(x_ref, gain_ref, w_ref, out_ref, q_ref, kt_ref, v_ref, mix_ref):
    inputs = x_ref[...].astype(jnp.float32)
    spread = jnp.mean(inputs * inputs, axis=-1, keepdims=True)
    normed = (inputs * lax.rsqrt(spread + epsilon) * gain_ref[...]).astype(jnp.bfloat16)
    q_ref[...] = jnp.dot(normed, w_ref[0], preferred_element_type=jnp.float32).astype(jnp.bfloat16)
    v_ref[...] = jnp.dot(normed, w_ref[2], preferred_element_type=jnp.float32).astype(jnp.bfloat16)
    kt_ref[...] = jnp.dot(normed, w_ref[1], preferred_element_type=jnp.float32).T.astype(jnp.bfloat16)
    width = inputs.shape[-1]
    head_size = width // ENC_HEADS
    scale = head_size ** (-0.5)
    pair = 2 * NLEN
    rows_of = lax.broadcasted_iota(jnp.int32, (pair, pair), 0) // NLEN
    cols_of = lax.broadcasted_iota(jnp.int32, (pair, pair), 1) // NLEN
    same = rows_of == cols_of
    for b in range(inputs.shape[0] // pair):
        rows = pl.ds(b * pair, pair)
        for h in range(ENC_HEADS):
            cols = pl.ds(h * head_size, head_size)
            scores = jnp.dot(q_ref[rows, cols], kt_ref[cols, rows], preferred_element_type=jnp.float32) * scale
            weights = _softmax_bf16(jnp.where(same, scores, -jnp.inf))
            mix_ref[rows, cols] = jnp.dot(
                weights, v_ref[rows, cols], preferred_element_type=jnp.float32
            ).astype(jnp.bfloat16)
    output = jnp.dot(mix_ref[...], w_ref[3], preferred_element_type=jnp.float32)
    out_ref[...] = (inputs + output).astype(jnp.bfloat16)


def encode_blocks(blocks, gain, attention, group=8):
    count, length, width = blocks.shape
    group = min(group, count)
    rows = group * length
    flat = blocks.reshape(count * length, width)
    return pl.pallas_call(
        _encoder_kernel,
        out_shape=jax.ShapeDtypeStruct(flat.shape, jnp.bfloat16),
        grid=(count // group,),
        in_specs=[
            pl.BlockSpec((rows, width), lambda i: (i, 0)),
            pl.BlockSpec((1, width), lambda i: (0, 0)),
            pl.BlockSpec(attention.shape, lambda i: (0, 0, 0)),
        ],
        out_specs=pl.BlockSpec((rows, width), lambda i: (i, 0)),
        scratch_shapes=[
            pltpu.VMEM((rows, width), jnp.bfloat16),
            pltpu.VMEM((width, rows), jnp.bfloat16),
            pltpu.VMEM((rows, width), jnp.bfloat16),
            pltpu.VMEM((rows, width), jnp.bfloat16),
        ],
    )(flat, gain.reshape(1, width), attention)


def _cross_kernel(q_ref, kt_ref, v_ref, out_ref):
    scale = HEAD_DIM ** (-0.5)
    memory = NEIGH * NLEN
    for s in range(q_ref.shape[0] // SPAN):
        rq = pl.ds(s * SPAN, SPAN)
        rk = pl.ds(s * memory, memory)
        for h in range(q_ref.shape[-1] // HEAD_DIM):
            cols = pl.ds(h * HEAD_DIM, HEAD_DIM)
            scores = jnp.dot(q_ref[rq, cols], kt_ref[cols, rk], preferred_element_type=jnp.float32) * scale
            weights = _softmax_bf16(scores)
            out_ref[rq, cols] = jnp.dot(
                weights, v_ref[rk, cols], preferred_element_type=jnp.float32
            ).astype(jnp.bfloat16)


def cross_attend(queries, keys_t, values, group=4):
    length, width = queries.shape
    memory = NEIGH * NLEN
    group = min(group, length // SPAN)
    return pl.pallas_call(
        _cross_kernel,
        out_shape=jax.ShapeDtypeStruct(queries.shape, jnp.bfloat16),
        grid=(length // (SPAN * group),),
        in_specs=[
            pl.BlockSpec((SPAN * group, width), lambda c: (c, 0)),
            pl.BlockSpec((width, memory * group), lambda c: (0, c)),
            pl.BlockSpec((memory * group, width), lambda c: (c, 0)),
        ],
        out_specs=pl.BlockSpec((SPAN * group, width), lambda c: (c, 0)),
    )(queries, keys_t, values)


def make_shards(n_seq):
    def shards(queries, neighbour_input, owner_list, block_list, enc_gain, enc_attn, kv_weight):
        owners = owner_list.reshape(-1)
        indices = block_list.reshape(-1)
        refs = owners.shape[0]
        per_owner = -(-refs // n_seq)
        same = owners[:, None] == owners[None, :]
        earlier = jnp.arange(refs)[None, :] < jnp.arange(refs)[:, None]
        rank = jnp.sum(same & earlier, axis=1).astype(jnp.int32)
        asks = jnp.stack([owners, indices, rank])
        asked = lax.all_gather(asks, "seq", axis=0, tiled=False)
        asked, enc_attn = lax.optimization_barrier((asked, enc_attn))
        full_weights = lax.all_gather(enc_attn, "dp", axis=1, tiled=True)
        me = lax.axis_index("seq")
        slots = jnp.arange(per_owner, dtype=jnp.int32)
        match = (asked[:, 0, None, :] == me) & (asked[:, 2, None, :] == slots[None, :, None])
        picks = jnp.sum(jnp.where(match, asked[:, 1, None, :], 0), axis=-1)
        sent = jnp.take(neighbour_input[0], picks.reshape(-1), axis=0, mode="clip")
        sent = sent.reshape(n_seq, per_owner, NLEN, neighbour_input.shape[-1])
        got = lax.all_to_all(sent, "seq", 0, 0, tiled=True)
        got = got.reshape(n_seq * per_owner, NLEN, neighbour_input.shape[-1])
        chosen_raw = jnp.take(got, owners * per_owner + rank, axis=0, mode="clip")
        chosen = encode_blocks(chosen_raw, enc_gain, full_weights)
        keys_t = jnp.einsum(
            "ef,re->fr", kv_weight[0], chosen, preferred_element_type=jnp.float32
        ).astype(jnp.bfloat16)
        values = jnp.dot(chosen, kv_weight[1], preferred_element_type=jnp.float32).astype(jnp.bfloat16)
        return cross_attend(queries[0], keys_t, values)[None]

    return shards


def solution(mesh):
    return jax.shard_map(
        make_shards(mesh.shape["seq"]),
        mesh=mesh,
        in_specs=(
            P("dp", "seq", None),
            P("dp", "seq", None, None),
            P("dp", "seq", None),
            P("dp", "seq", None),
            P(),
            P(None, "dp", None),
            P(),
        ),
        out_specs=P("dp", "seq", None),
        check_vma=False,
    )
```

```python
import jax
import jax.numpy as jnp
from jax import lax
from jax.experimental import pallas as pl
from jax.experimental.pallas import tpu as pltpu
from jax.sharding import PartitionSpec as P

HEADS = 16
HEAD_DIM = 128
ENC_HEADS = 7
NLEN = 64
SPAN = 64
NEIGH = 2
NB_DEV = 4


epsilon = 1e-05


def _softmax_bf16(scores):
    highest = jnp.max(scores, axis=-1, keepdims=True)
    raised = jnp.exp(scores - highest)
    return (raised * (1.0 / jnp.sum(raised, axis=-1, keepdims=True))).astype(jnp.bfloat16)


def _encoder_kernel(x_ref, gain_ref, w_ref, out_ref, q_ref, kt_ref, v_ref, mix_ref):
    inputs = x_ref[...].astype(jnp.float32)
    spread = jnp.mean(inputs * inputs, axis=-1, keepdims=True)
    normed = (inputs * lax.rsqrt(spread + epsilon) * gain_ref[...]).astype(jnp.bfloat16)
    q_ref[...] = jnp.dot(normed, w_ref[0], preferred_element_type=jnp.float32).astype(jnp.bfloat16)
    v_ref[...] = jnp.dot(normed, w_ref[2], preferred_element_type=jnp.float32).astype(jnp.bfloat16)
    kt_ref[...] = jnp.dot(normed, w_ref[1], preferred_element_type=jnp.float32).T.astype(jnp.bfloat16)
    width = inputs.shape[-1]
    head_size = width // ENC_HEADS
    scale = head_size ** (-0.5)
    pair = 2 * NLEN
    rows_of = lax.broadcasted_iota(jnp.int32, (pair, pair), 0) // NLEN
    cols_of = lax.broadcasted_iota(jnp.int32, (pair, pair), 1) // NLEN
    same = rows_of == cols_of
    for b in range(inputs.shape[0] // pair):
        rows = pl.ds(b * pair, pair)
        for h in range(ENC_HEADS):
            cols = pl.ds(h * head_size, head_size)
            scores = jnp.dot(q_ref[rows, cols], kt_ref[cols, rows], preferred_element_type=jnp.float32) * scale
            weights = _softmax_bf16(jnp.where(same, scores, -jnp.inf))
            mix_ref[rows, cols] = jnp.dot(
                weights, v_ref[rows, cols], preferred_element_type=jnp.float32
            ).astype(jnp.bfloat16)
    output = jnp.dot(mix_ref[...], w_ref[3], preferred_element_type=jnp.float32)
    out_ref[...] = (inputs + output).astype(jnp.bfloat16)


def encode_blocks(blocks, gain, attention, group=8):
    count, length, width = blocks.shape
    group = min(group, count)
    rows = group * length
    flat = blocks.reshape(count * length, width)
    return pl.pallas_call(
        _encoder_kernel,
        out_shape=jax.ShapeDtypeStruct(flat.shape, jnp.bfloat16),
        grid=(count // group,),
        in_specs=[
            pl.BlockSpec((rows, width), lambda i: (i, 0)),
            pl.BlockSpec((1, width), lambda i: (0, 0)),
            pl.BlockSpec(attention.shape, lambda i: (0, 0, 0)),
        ],
        out_specs=pl.BlockSpec((rows, width), lambda i: (i, 0)),
        scratch_shapes=[
            pltpu.VMEM((rows, width), jnp.bfloat16),
            pltpu.VMEM((width, rows), jnp.bfloat16),
            pltpu.VMEM((rows, width), jnp.bfloat16),
            pltpu.VMEM((rows, width), jnp.bfloat16),
        ],
    )(flat, gain.reshape(1, width), attention)


def _cross_kernel(q_ref, kt_ref, v_ref, out_ref):
    scale = HEAD_DIM ** (-0.5)
    memory = NEIGH * NLEN
    for s in range(q_ref.shape[0] // SPAN):
        rq = pl.ds(s * SPAN, SPAN)
        rk = pl.ds(s * memory, memory)
        for h in range(q_ref.shape[-1] // HEAD_DIM):
            cols = pl.ds(h * HEAD_DIM, HEAD_DIM)
            scores = jnp.dot(q_ref[rq, cols], kt_ref[cols, rk], preferred_element_type=jnp.float32) * scale
            weights = _softmax_bf16(scores)
            out_ref[rq, cols] = jnp.dot(
                weights, v_ref[rk, cols], preferred_element_type=jnp.float32
            ).astype(jnp.bfloat16)


def cross_attend(queries, keys_t, values, group=4):
    length, width = queries.shape
    memory = NEIGH * NLEN
    group = min(group, length // SPAN)
    return pl.pallas_call(
        _cross_kernel,
        out_shape=jax.ShapeDtypeStruct(queries.shape, jnp.bfloat16),
        grid=(length // (SPAN * group),),
        in_specs=[
            pl.BlockSpec((SPAN * group, width), lambda c: (c, 0)),
            pl.BlockSpec((width, memory * group), lambda c: (0, c)),
            pl.BlockSpec((memory * group, width), lambda c: (c, 0)),
        ],
        out_specs=pl.BlockSpec((SPAN * group, width), lambda c: (c, 0)),
    )(queries, keys_t, values)


def make_shards(n_seq):
    def shards(queries, neighbour_input, owner_list, block_list, enc_gain, enc_attn, kv_weight):
        full_weights = lax.all_gather(enc_attn, "dp", axis=1, tiled=True)
        me = lax.axis_index("seq")
        owners = owner_list.reshape(-1)
        indices = block_list.reshape(-1)
        refs = owners.shape[0]
        per_owner = -(-refs // n_seq)
        same = owners[:, None] == owners[None, :]
        earlier = jnp.arange(refs)[None, :] < jnp.arange(refs)[:, None]
        rank = jnp.sum(same & earlier, axis=1).astype(jnp.int32)
        asks = jnp.stack([owners, indices, rank])
        shifted = [asks]
        for shift in range(1, n_seq):
            ring = [(src, (src + shift) % n_seq) for src in range(n_seq)]
            shifted.append(lax.ppermute(asks, "seq", ring))
        shifted = jnp.stack(shifted)
        asked = jnp.take(shifted, (me - jnp.arange(n_seq)) % n_seq, axis=0)
        slots = jnp.arange(per_owner, dtype=jnp.int32)
        match = (asked[:, 0, None, :] == me) & (asked[:, 2, None, :] == slots[None, :, None])
        picks = jnp.sum(jnp.where(match, asked[:, 1, None, :], 0), axis=-1)
        sent = jnp.take(neighbour_input[0], picks.reshape(-1), axis=0, mode="clip")
        sent = sent.reshape(n_seq, per_owner, NLEN, neighbour_input.shape[-1])
        got = lax.all_to_all(sent, "seq", 0, 0, tiled=True)
        got = got.reshape(n_seq * per_owner, NLEN, neighbour_input.shape[-1])
        chosen_raw = jnp.take(got, owners * per_owner + rank, axis=0, mode="clip")
        chosen = encode_blocks(chosen_raw, enc_gain, full_weights)
        keys_t = jnp.einsum(
            "ef,re->fr", kv_weight[0], chosen, preferred_element_type=jnp.float32
        ).astype(jnp.bfloat16)
        values = jnp.dot(chosen, kv_weight[1], preferred_element_type=jnp.float32).astype(jnp.bfloat16)
        return cross_attend(queries[0], keys_t, values)[None]

    return shards


def solution(mesh):
    return jax.shard_map(
        make_shards(mesh.shape["seq"]),
        mesh=mesh,
        in_specs=(
            P("dp", "seq", None),
            P("dp", "seq", None, None),
            P("dp", "seq", None),
            P("dp", "seq", None),
            P(),
            P(None, "dp", None),
            P(),
        ),
        out_specs=P("dp", "seq", None),
        check_vma=False,
    )
```

```python
import jax
import jax.numpy as jnp
from jax import lax
from jax.experimental import pallas as pl
from jax.experimental.pallas import tpu as pltpu
from jax.sharding import PartitionSpec as P

HEADS = 16
HEAD_DIM = 128
ENC_HEADS = 7
NLEN = 64
SPAN = 64
NEIGH = 2
NB_DEV = 4


epsilon = 1e-05


def _softmax_bf16(scores):
    highest = jnp.max(scores, axis=-1, keepdims=True)
    raised = jnp.exp(scores - highest)
    return (raised * (1.0 / jnp.sum(raised, axis=-1, keepdims=True))).astype(jnp.bfloat16)


def _encoder_kernel(x_ref, gain_ref, w_ref, out_ref, q_ref, kt_ref, v_ref, mix_ref):
    inputs = x_ref[...].astype(jnp.float32)
    spread = jnp.mean(inputs * inputs, axis=-1, keepdims=True)
    normed = (inputs * lax.rsqrt(spread + epsilon) * gain_ref[...]).astype(jnp.bfloat16)
    q_ref[...] = jnp.dot(normed, w_ref[0], preferred_element_type=jnp.float32).astype(jnp.bfloat16)
    v_ref[...] = jnp.dot(normed, w_ref[2], preferred_element_type=jnp.float32).astype(jnp.bfloat16)
    kt_ref[...] = jnp.dot(normed, w_ref[1], preferred_element_type=jnp.float32).T.astype(jnp.bfloat16)
    width = inputs.shape[-1]
    head_size = width // ENC_HEADS
    scale = head_size ** (-0.5)
    pair = 2 * NLEN
    rows_of = lax.broadcasted_iota(jnp.int32, (pair, pair), 0) // NLEN
    cols_of = lax.broadcasted_iota(jnp.int32, (pair, pair), 1) // NLEN
    same = rows_of == cols_of
    for b in range(inputs.shape[0] // pair):
        rows = pl.ds(b * pair, pair)
        for h in range(ENC_HEADS):
            cols = pl.ds(h * head_size, head_size)
            scores = jnp.dot(q_ref[rows, cols], kt_ref[cols, rows], preferred_element_type=jnp.float32) * scale
            weights = _softmax_bf16(jnp.where(same, scores, -jnp.inf))
            mix_ref[rows, cols] = jnp.dot(
                weights, v_ref[rows, cols], preferred_element_type=jnp.float32
            ).astype(jnp.bfloat16)
    output = jnp.dot(mix_ref[...], w_ref[3], preferred_element_type=jnp.float32)
    out_ref[...] = (inputs + output).astype(jnp.bfloat16)


def encode_blocks(blocks, gain, attention, group=8):
    count, length, width = blocks.shape
    group = min(group, count)
    rows = group * length
    flat = blocks.reshape(count * length, width)
    return pl.pallas_call(
        _encoder_kernel,
        out_shape=jax.ShapeDtypeStruct(flat.shape, jnp.bfloat16),
        grid=(count // group,),
        in_specs=[
            pl.BlockSpec((rows, width), lambda i: (i, 0)),
            pl.BlockSpec((1, width), lambda i: (0, 0)),
            pl.BlockSpec(attention.shape, lambda i: (0, 0, 0)),
        ],
        out_specs=pl.BlockSpec((rows, width), lambda i: (i, 0)),
        scratch_shapes=[
            pltpu.VMEM((rows, width), jnp.bfloat16),
            pltpu.VMEM((width, rows), jnp.bfloat16),
            pltpu.VMEM((rows, width), jnp.bfloat16),
            pltpu.VMEM((rows, width), jnp.bfloat16),
        ],
    )(flat, gain.reshape(1, width), attention)


def _cross_kernel(q_ref, kt_ref, v_ref, out_ref):
    scale = HEAD_DIM ** (-0.5)
    memory = NEIGH * NLEN
    for s in range(q_ref.shape[0] // SPAN):
        rq = pl.ds(s * SPAN, SPAN)
        rk = pl.ds(s * memory, memory)
        for h in range(q_ref.shape[-1] // HEAD_DIM):
            cols = pl.ds(h * HEAD_DIM, HEAD_DIM)
            scores = jnp.dot(q_ref[rq, cols], kt_ref[cols, rk], preferred_element_type=jnp.float32) * scale
            weights = _softmax_bf16(scores)
            out_ref[rq, cols] = jnp.dot(
                weights, v_ref[rk, cols], preferred_element_type=jnp.float32
            ).astype(jnp.bfloat16)


def cross_attend(queries, keys_t, values, group=4):
    length, width = queries.shape
    memory = NEIGH * NLEN
    group = min(group, length // SPAN)
    return pl.pallas_call(
        _cross_kernel,
        out_shape=jax.ShapeDtypeStruct(queries.shape, jnp.bfloat16),
        grid=(length // (SPAN * group),),
        in_specs=[
            pl.BlockSpec((SPAN * group, width), lambda c: (c, 0)),
            pl.BlockSpec((width, memory * group), lambda c: (0, c)),
            pl.BlockSpec((memory * group, width), lambda c: (c, 0)),
        ],
        out_specs=pl.BlockSpec((SPAN * group, width), lambda c: (c, 0)),
    )(queries, keys_t, values)


def make_shards(n_seq):
    def shards(queries, neighbour_input, owner_list, block_list, enc_gain, enc_attn, kv_weight):
        full_weights = lax.all_gather(enc_attn, "dp", axis=1, tiled=True)
        me = lax.axis_index("seq")
        owners = owner_list.reshape(-1)
        indices = block_list.reshape(-1)
        refs = owners.shape[0]
        per_owner = -(-refs // n_seq)
        same = owners[:, None] == owners[None, :]
        earlier = jnp.arange(refs)[None, :] < jnp.arange(refs)[:, None]
        rank = jnp.sum(same & earlier, axis=1).astype(jnp.int32)
        asks = jnp.stack([owners, indices, rank])
        asks = jnp.broadcast_to(asks[None], (n_seq, 3, refs))
        asked = lax.all_to_all(asks, "seq", 0, 0, tiled=True)
        slots = jnp.arange(per_owner, dtype=jnp.int32)
        match = (asked[:, 0, None, :] == me) & (asked[:, 2, None, :] == slots[None, :, None])
        picks = jnp.sum(jnp.where(match, asked[:, 1, None, :], 0), axis=-1)
        sent = jnp.take(neighbour_input[0], picks.reshape(-1), axis=0, mode="clip")
        sent = sent.reshape(n_seq, per_owner, NLEN, neighbour_input.shape[-1])
        got = lax.all_to_all(sent, "seq", 0, 0, tiled=True)
        got = got.reshape(n_seq * per_owner, NLEN, neighbour_input.shape[-1])
        chosen_raw = jnp.take(got, owners * per_owner + rank, axis=0, mode="clip")
        chosen = encode_blocks(chosen_raw, enc_gain, full_weights)
        key_value = jnp.einsum(
            "re,pef->prf", chosen, kv_weight, preferred_element_type=jnp.float32
        ).astype(jnp.bfloat16)
        keys_t = key_value[0].T
        values = key_value[1]
        return cross_attend(queries[0], keys_t, values)[None]

    return shards


def solution(mesh):
    return jax.shard_map(
        make_shards(mesh.shape["seq"]),
        mesh=mesh,
        in_specs=(
            P("dp", "seq", None),
            P("dp", "seq", None, None),
            P("dp", "seq", None),
            P("dp", "seq", None),
            P(),
            P(None, "dp", None),
            P(),
        ),
        out_specs=P("dp", "seq", None),
        check_vma=False,
    )
```

```python
import jax
import jax.numpy as jnp
from jax import lax
from jax.experimental import pallas as pl
from jax.experimental.pallas import tpu as pltpu
from jax.sharding import PartitionSpec as P

HEADS = 16
HEAD_DIM = 128
ENC_HEADS = 7
NLEN = 64
SPAN = 64
NEIGH = 2
NB_DEV = 4


epsilon = 1e-05


def _softmax_bf16(scores):
    highest = jnp.max(scores, axis=-1, keepdims=True)
    raised = jnp.exp(scores - highest)
    return (raised * (1.0 / jnp.sum(raised, axis=-1, keepdims=True))).astype(jnp.bfloat16)


def _encoder_kernel(x_ref, gain_ref, w_ref, out_ref, q_ref, kt_ref, v_ref, mix_ref):
    inputs = x_ref[...].astype(jnp.float32)
    spread = jnp.mean(inputs * inputs, axis=-1, keepdims=True)
    normed = (inputs * lax.rsqrt(spread + epsilon) * gain_ref[...]).astype(jnp.bfloat16)
    q_ref[...] = jnp.dot(normed, w_ref[0], preferred_element_type=jnp.float32).astype(jnp.bfloat16)
    v_ref[...] = jnp.dot(normed, w_ref[2], preferred_element_type=jnp.float32).astype(jnp.bfloat16)
    kt_ref[...] = jnp.dot(normed, w_ref[1], preferred_element_type=jnp.float32).T.astype(jnp.bfloat16)
    width = inputs.shape[-1]
    head_size = width // ENC_HEADS
    scale = head_size ** (-0.5)
    pair = 2 * NLEN
    rows_of = lax.broadcasted_iota(jnp.int32, (pair, pair), 0) // NLEN
    cols_of = lax.broadcasted_iota(jnp.int32, (pair, pair), 1) // NLEN
    same = rows_of == cols_of
    for b in range(inputs.shape[0] // pair):
        rows = pl.ds(b * pair, pair)
        for h in range(ENC_HEADS):
            cols = pl.ds(h * head_size, head_size)
            scores = jnp.dot(q_ref[rows, cols], kt_ref[cols, rows], preferred_element_type=jnp.float32) * scale
            weights = _softmax_bf16(jnp.where(same, scores, -jnp.inf))
            mix_ref[rows, cols] = jnp.dot(
                weights, v_ref[rows, cols], preferred_element_type=jnp.float32
            ).astype(jnp.bfloat16)
    output = jnp.dot(mix_ref[...], w_ref[3], preferred_element_type=jnp.float32)
    out_ref[...] = (inputs + output).astype(jnp.bfloat16)


def encode_blocks(blocks, gain, attention, group=8):
    count, length, width = blocks.shape
    group = min(group, count)
    rows = group * length
    flat = blocks.reshape(count * length, width)
    return pl.pallas_call(
        _encoder_kernel,
        out_shape=jax.ShapeDtypeStruct(flat.shape, jnp.bfloat16),
        grid=(count // group,),
        in_specs=[
            pl.BlockSpec((rows, width), lambda i: (i, 0)),
            pl.BlockSpec((1, width), lambda i: (0, 0)),
            pl.BlockSpec(attention.shape, lambda i: (0, 0, 0)),
        ],
        out_specs=pl.BlockSpec((rows, width), lambda i: (i, 0)),
        scratch_shapes=[
            pltpu.VMEM((rows, width), jnp.bfloat16),
            pltpu.VMEM((width, rows), jnp.bfloat16),
            pltpu.VMEM((rows, width), jnp.bfloat16),
            pltpu.VMEM((rows, width), jnp.bfloat16),
        ],
    )(flat, gain.reshape(1, width), attention)


def _cross_kernel(q_ref, kt_ref, v_ref, out_ref):
    scale = HEAD_DIM ** (-0.5)
    memory = NEIGH * NLEN
    for s in range(q_ref.shape[0] // SPAN):
        rq = pl.ds(s * SPAN, SPAN)
        rk = pl.ds(s * memory, memory)
        for h in range(q_ref.shape[-1] // HEAD_DIM):
            cols = pl.ds(h * HEAD_DIM, HEAD_DIM)
            scores = jnp.dot(q_ref[rq, cols], kt_ref[cols, rk], preferred_element_type=jnp.float32) * scale
            weights = _softmax_bf16(scores)
            out_ref[rq, cols] = jnp.dot(
                weights, v_ref[rk, cols], preferred_element_type=jnp.float32
            ).astype(jnp.bfloat16)


def cross_attend(queries, keys_t, values, group=4):
    length, width = queries.shape
    memory = NEIGH * NLEN
    group = min(group, length // SPAN)
    return pl.pallas_call(
        _cross_kernel,
        out_shape=jax.ShapeDtypeStruct(queries.shape, jnp.bfloat16),
        grid=(length // (SPAN * group),),
        in_specs=[
            pl.BlockSpec((SPAN * group, width), lambda c: (c, 0)),
            pl.BlockSpec((width, memory * group), lambda c: (0, c)),
            pl.BlockSpec((memory * group, width), lambda c: (c, 0)),
        ],
        out_specs=pl.BlockSpec((SPAN * group, width), lambda c: (c, 0)),
    )(queries, keys_t, values)


def gather_weights(shard, n_dp):
    n_x = n_dp // 2
    place = lax.axis_index("dp")
    x, core = place // 2, place % 2
    pieces = [shard]
    for shift in range(1, n_x):
        ring = [(src, ((src // 2 + shift) % n_x) * 2 + src % 2) for src in range(n_dp)]
        pieces.append(lax.ppermute(shard, "dp", ring))
    mine = jnp.stack(pieces)
    other = lax.ppermute(mine, "dp", [(src, src ^ 1) for src in range(n_dp)])
    order = (x - jnp.arange(n_x)) % n_x
    mine = jnp.take(mine, order, axis=0)
    other = jnp.take(other, order, axis=0)
    both = jnp.where(core == 0, jnp.stack([mine, other], 1), jnp.stack([other, mine], 1))
    count, rows, width = shard.shape
    return both.transpose(2, 0, 1, 3, 4).reshape(count, n_dp * rows, width)


def make_shards(n_seq, n_dp):
    def shards(queries, neighbour_input, owner_list, block_list, enc_gain, enc_attn, kv_weight):
        full_weights = gather_weights(enc_attn, n_dp)
        me = lax.axis_index("seq")
        owners = owner_list.reshape(-1)
        indices = block_list.reshape(-1)
        refs = owners.shape[0]
        per_owner = -(-refs // n_seq)
        same = owners[:, None] == owners[None, :]
        earlier = jnp.arange(refs)[None, :] < jnp.arange(refs)[:, None]
        rank = jnp.sum(same & earlier, axis=1).astype(jnp.int32)
        asks = jnp.stack([owners, indices, rank])
        asks = jnp.broadcast_to(asks[None], (n_seq, 3, refs))
        asked = lax.all_to_all(asks, "seq", 0, 0, tiled=True)
        slots = jnp.arange(per_owner, dtype=jnp.int32)
        match = (asked[:, 0, None, :] == me) & (asked[:, 2, None, :] == slots[None, :, None])
        picks = jnp.sum(jnp.where(match, asked[:, 1, None, :], 0), axis=-1)
        sent = jnp.take(neighbour_input[0], picks.reshape(-1), axis=0, mode="clip")
        sent = sent.reshape(n_seq, per_owner, NLEN, neighbour_input.shape[-1])
        got = lax.all_to_all(sent, "seq", 0, 0, tiled=True)
        got = got.reshape(n_seq * per_owner, NLEN, neighbour_input.shape[-1])
        chosen_raw = jnp.take(got, owners * per_owner + rank, axis=0, mode="clip")
        chosen = encode_blocks(chosen_raw, enc_gain, full_weights)
        keys_t = jnp.einsum(
            "ef,re->fr", kv_weight[0], chosen, preferred_element_type=jnp.float32
        ).astype(jnp.bfloat16)
        values = jnp.dot(chosen, kv_weight[1], preferred_element_type=jnp.float32).astype(jnp.bfloat16)
        return cross_attend(queries[0], keys_t, values)[None]

    return shards


def solution(mesh):
    return jax.shard_map(
        make_shards(mesh.shape["seq"], mesh.shape["dp"]),
        mesh=mesh,
        in_specs=(
            P("dp", "seq", None),
            P("dp", "seq", None, None),
            P("dp", "seq", None),
            P("dp", "seq", None),
            P(),
            P(None, "dp", None),
            P(),
        ),
        out_specs=P("dp", "seq", None),
        check_vma=False,
    )
```

```python
import jax
import jax.numpy as jnp
from jax import lax
from jax.experimental import pallas as pl
from jax.experimental.pallas import tpu as pltpu
from jax.sharding import PartitionSpec as P

HEADS = 16
HEAD_DIM = 128
ENC_HEADS = 7
NLEN = 64
SPAN = 64
NEIGH = 2
NB_DEV = 4


epsilon = 1e-05


def _softmax_bf16(scores):
    highest = jnp.max(scores, axis=-1, keepdims=True)
    raised = jnp.exp(scores - highest)
    return (raised * (1.0 / jnp.sum(raised, axis=-1, keepdims=True))).astype(jnp.bfloat16)


def _encoder_kernel(x_ref, gain_ref, w_ref, out_ref, q_ref, kt_ref, v_ref, mix_ref):
    inputs = x_ref[...].astype(jnp.float32)
    spread = jnp.mean(inputs * inputs, axis=-1, keepdims=True)
    normed = (inputs * lax.rsqrt(spread + epsilon) * gain_ref[...]).astype(jnp.bfloat16)
    q_ref[...] = jnp.dot(normed, w_ref[0], preferred_element_type=jnp.float32).astype(jnp.bfloat16)
    v_ref[...] = jnp.dot(normed, w_ref[2], preferred_element_type=jnp.float32).astype(jnp.bfloat16)
    kt_ref[...] = jnp.dot(normed, w_ref[1], preferred_element_type=jnp.float32).T.astype(jnp.bfloat16)
    width = inputs.shape[-1]
    head_size = width // ENC_HEADS
    scale = head_size ** (-0.5)
    pair = 2 * NLEN
    rows_of = lax.broadcasted_iota(jnp.int32, (pair, pair), 0) // NLEN
    cols_of = lax.broadcasted_iota(jnp.int32, (pair, pair), 1) // NLEN
    same = rows_of == cols_of
    for b in range(inputs.shape[0] // pair):
        rows = pl.ds(b * pair, pair)
        for h in range(ENC_HEADS):
            cols = pl.ds(h * head_size, head_size)
            scores = jnp.dot(q_ref[rows, cols], kt_ref[cols, rows], preferred_element_type=jnp.float32) * scale
            weights = _softmax_bf16(jnp.where(same, scores, -jnp.inf))
            mix_ref[rows, cols] = jnp.dot(
                weights, v_ref[rows, cols], preferred_element_type=jnp.float32
            ).astype(jnp.bfloat16)
    output = jnp.dot(mix_ref[...], w_ref[3], preferred_element_type=jnp.float32)
    out_ref[...] = (inputs + output).astype(jnp.bfloat16)


def encode_blocks(blocks, gain, attention, group=8):
    count, length, width = blocks.shape
    group = min(group, count)
    rows = group * length
    flat = blocks.reshape(count * length, width)
    return pl.pallas_call(
        _encoder_kernel,
        out_shape=jax.ShapeDtypeStruct(flat.shape, jnp.bfloat16),
        grid=(count // group,),
        in_specs=[
            pl.BlockSpec((rows, width), lambda i: (i, 0)),
            pl.BlockSpec((1, width), lambda i: (0, 0)),
            pl.BlockSpec(attention.shape, lambda i: (0, 0, 0)),
        ],
        out_specs=pl.BlockSpec((rows, width), lambda i: (i, 0)),
        scratch_shapes=[
            pltpu.VMEM((rows, width), jnp.bfloat16),
            pltpu.VMEM((width, rows), jnp.bfloat16),
            pltpu.VMEM((rows, width), jnp.bfloat16),
            pltpu.VMEM((rows, width), jnp.bfloat16),
        ],
    )(flat, gain.reshape(1, width), attention)


def _cross_kernel(q_ref, kt_ref, v_ref, out_ref):
    scale = HEAD_DIM ** (-0.5)
    memory = NEIGH * NLEN
    for s in range(q_ref.shape[0] // SPAN):
        rq = pl.ds(s * SPAN, SPAN)
        rk = pl.ds(s * memory, memory)
        for h in range(q_ref.shape[-1] // HEAD_DIM):
            cols = pl.ds(h * HEAD_DIM, HEAD_DIM)
            scores = jnp.dot(q_ref[rq, cols], kt_ref[cols, rk], preferred_element_type=jnp.float32) * scale
            weights = _softmax_bf16(scores)
            out_ref[rq, cols] = jnp.dot(
                weights, v_ref[rk, cols], preferred_element_type=jnp.float32
            ).astype(jnp.bfloat16)


def cross_attend(queries, keys_t, values, group=4):
    length, width = queries.shape
    memory = NEIGH * NLEN
    group = min(group, length // SPAN)
    return pl.pallas_call(
        _cross_kernel,
        out_shape=jax.ShapeDtypeStruct(queries.shape, jnp.bfloat16),
        grid=(length // (SPAN * group),),
        in_specs=[
            pl.BlockSpec((SPAN * group, width), lambda c: (c, 0)),
            pl.BlockSpec((width, memory * group), lambda c: (0, c)),
            pl.BlockSpec((memory * group, width), lambda c: (c, 0)),
        ],
        out_specs=pl.BlockSpec((SPAN * group, width), lambda c: (c, 0)),
    )(queries, keys_t, values)


def gather_weights(shard, n_dp):
    n_x = n_dp // 2
    place = lax.axis_index("dp")
    x, core = place // 2, place % 2
    pieces = [(shard, place)]
    for shift in range(1, n_x):
        ring = [(src, ((src // 2 + shift) % n_x) * 2 + src % 2) for src in range(n_dp)]
        pieces.append((lax.ppermute(shard, "dp", ring), ((x - shift) % n_x) * 2 + core))
    swap = [(src, src ^ 1) for src in range(n_dp)]
    pieces += [(lax.ppermute(piece, "dp", swap), owner ^ 1) for piece, owner in pieces]
    count, rows, width = shard.shape
    full = jnp.zeros((count, n_dp * rows, width), shard.dtype)
    for piece, owner in pieces:
        full = lax.dynamic_update_slice(full, piece, (0, owner * rows, 0))
    return full


def make_shards(n_seq, n_dp):
    def shards(queries, neighbour_input, owner_list, block_list, enc_gain, enc_attn, kv_weight):
        full_weights = gather_weights(enc_attn, n_dp)
        me = lax.axis_index("seq")
        owners = owner_list.reshape(-1)
        indices = block_list.reshape(-1)
        refs = owners.shape[0]
        per_owner = -(-refs // n_seq)
        same = owners[:, None] == owners[None, :]
        earlier = jnp.arange(refs)[None, :] < jnp.arange(refs)[:, None]
        rank = jnp.sum(same & earlier, axis=1).astype(jnp.int32)
        asks = jnp.stack([owners, indices, rank])
        asks = jnp.broadcast_to(asks[None], (n_seq, 3, refs))
        asked = lax.all_to_all(asks, "seq", 0, 0, tiled=True)
        slots = jnp.arange(per_owner, dtype=jnp.int32)
        match = (asked[:, 0, None, :] == me) & (asked[:, 2, None, :] == slots[None, :, None])
        picks = jnp.sum(jnp.where(match, asked[:, 1, None, :], 0), axis=-1)
        sent = jnp.take(neighbour_input[0], picks.reshape(-1), axis=0, mode="clip")
        sent = sent.reshape(n_seq, per_owner, NLEN, neighbour_input.shape[-1])
        got = lax.all_to_all(sent, "seq", 0, 0, tiled=True)
        got = got.reshape(n_seq * per_owner, NLEN, neighbour_input.shape[-1])
        chosen_raw = jnp.take(got, owners * per_owner + rank, axis=0, mode="clip")
        chosen = encode_blocks(chosen_raw, enc_gain, full_weights)
        keys_t = jnp.einsum(
            "ef,re->fr", kv_weight[0], chosen, preferred_element_type=jnp.float32
        ).astype(jnp.bfloat16)
        values = jnp.dot(chosen, kv_weight[1], preferred_element_type=jnp.float32).astype(jnp.bfloat16)
        return cross_attend(queries[0], keys_t, values)[None]

    return shards


def solution(mesh):
    return jax.shard_map(
        make_shards(mesh.shape["seq"], mesh.shape["dp"]),
        mesh=mesh,
        in_specs=(
            P("dp", "seq", None),
            P("dp", "seq", None, None),
            P("dp", "seq", None),
            P("dp", "seq", None),
            P(),
            P(None, "dp", None),
            P(),
        ),
        out_specs=P("dp", "seq", None),
        check_vma=False,
    )
```

```python
import jax
import jax.numpy as jnp
from jax import lax
from jax.experimental import pallas as pl
from jax.experimental.pallas import tpu as pltpu
from jax.sharding import PartitionSpec as P

HEADS = 16
HEAD_DIM = 128
ENC_HEADS = 7
NLEN = 64
SPAN = 64
NEIGH = 2
NB_DEV = 4


epsilon = 1e-05


def _softmax_bf16(scores):
    highest = jnp.max(scores, axis=-1, keepdims=True)
    raised = jnp.exp(scores - highest)
    return (raised * (1.0 / jnp.sum(raised, axis=-1, keepdims=True))).astype(jnp.bfloat16)


def _encoder_kernel(x_ref, gain_ref, w_ref, out_ref, q_ref, kt_ref, v_ref, mix_ref):
    inputs = x_ref[...].astype(jnp.float32)
    spread = jnp.mean(inputs * inputs, axis=-1, keepdims=True)
    normed = (inputs * lax.rsqrt(spread + epsilon) * gain_ref[...]).astype(jnp.bfloat16)
    q_ref[...] = jnp.dot(normed, w_ref[0], preferred_element_type=jnp.float32).astype(jnp.bfloat16)
    v_ref[...] = jnp.dot(normed, w_ref[2], preferred_element_type=jnp.float32).astype(jnp.bfloat16)
    kt_ref[...] = jnp.dot(normed, w_ref[1], preferred_element_type=jnp.float32).T.astype(jnp.bfloat16)
    width = inputs.shape[-1]
    head_size = width // ENC_HEADS
    scale = head_size ** (-0.5)
    pair = 2 * NLEN
    rows_of = lax.broadcasted_iota(jnp.int32, (pair, pair), 0) // NLEN
    cols_of = lax.broadcasted_iota(jnp.int32, (pair, pair), 1) // NLEN
    same = rows_of == cols_of
    for b in range(inputs.shape[0] // pair):
        rows = pl.ds(b * pair, pair)
        for h in range(ENC_HEADS):
            cols = pl.ds(h * head_size, head_size)
            scores = jnp.dot(q_ref[rows, cols], kt_ref[cols, rows], preferred_element_type=jnp.float32) * scale
            weights = _softmax_bf16(jnp.where(same, scores, -jnp.inf))
            mix_ref[rows, cols] = jnp.dot(
                weights, v_ref[rows, cols], preferred_element_type=jnp.float32
            ).astype(jnp.bfloat16)
    output = jnp.dot(mix_ref[...], w_ref[3], preferred_element_type=jnp.float32)
    out_ref[...] = (inputs + output).astype(jnp.bfloat16)


def encode_blocks(blocks, gain, attention, group=8):
    count, length, width = blocks.shape
    group = min(group, count)
    rows = group * length
    flat = blocks.reshape(count * length, width)
    return pl.pallas_call(
        _encoder_kernel,
        out_shape=jax.ShapeDtypeStruct(flat.shape, jnp.bfloat16),
        grid=(count // group,),
        in_specs=[
            pl.BlockSpec((rows, width), lambda i: (i, 0)),
            pl.BlockSpec((1, width), lambda i: (0, 0)),
            pl.BlockSpec(attention.shape, lambda i: (0, 0, 0)),
        ],
        out_specs=pl.BlockSpec((rows, width), lambda i: (i, 0)),
        scratch_shapes=[
            pltpu.VMEM((rows, width), jnp.bfloat16),
            pltpu.VMEM((width, rows), jnp.bfloat16),
            pltpu.VMEM((rows, width), jnp.bfloat16),
            pltpu.VMEM((rows, width), jnp.bfloat16),
        ],
    )(flat, gain.reshape(1, width), attention)


def _cross_kernel(q_ref, kt_ref, v_ref, out_ref):
    scale = HEAD_DIM ** (-0.5)
    memory = NEIGH * NLEN
    for s in range(q_ref.shape[0] // SPAN):
        rq = pl.ds(s * SPAN, SPAN)
        rk = pl.ds(s * memory, memory)
        for h in range(q_ref.shape[-1] // HEAD_DIM):
            cols = pl.ds(h * HEAD_DIM, HEAD_DIM)
            scores = jnp.dot(q_ref[rq, cols], kt_ref[cols, rk], preferred_element_type=jnp.float32) * scale
            weights = _softmax_bf16(scores)
            out_ref[rq, cols] = jnp.dot(
                weights, v_ref[rk, cols], preferred_element_type=jnp.float32
            ).astype(jnp.bfloat16)


def cross_attend(queries, keys_t, values, group=4):
    length, width = queries.shape
    memory = NEIGH * NLEN
    group = min(group, length // SPAN)
    return pl.pallas_call(
        _cross_kernel,
        out_shape=jax.ShapeDtypeStruct(queries.shape, jnp.bfloat16),
        grid=(length // (SPAN * group),),
        in_specs=[
            pl.BlockSpec((SPAN * group, width), lambda c: (c, 0)),
            pl.BlockSpec((width, memory * group), lambda c: (0, c)),
            pl.BlockSpec((memory * group, width), lambda c: (c, 0)),
        ],
        out_specs=pl.BlockSpec((SPAN * group, width), lambda c: (c, 0)),
    )(queries, keys_t, values)


def gather_weights(shard, n_dp):
    n_x = n_dp // 2
    place = lax.axis_index("dp")
    x, core = place // 2, place % 2
    pieces = [(shard, place)]
    for shift in range(1, n_x):
        ring = [(src, ((src // 2 + shift) % n_x) * 2 + src % 2) for src in range(n_dp)]
        pieces.append((lax.ppermute(shard, "dp", ring), ((x - shift) % n_x) * 2 + core))
    swap = [(src, src ^ 1) for src in range(n_dp)]
    pieces += [(lax.ppermute(piece, "dp", swap), owner ^ 1) for piece, owner in pieces]
    count, rows, width = shard.shape
    full = jnp.zeros((count, n_dp * rows, width), shard.dtype)
    for piece, owner in pieces:
        full = lax.dynamic_update_slice(full, piece, (0, owner * rows, 0))
    return full


def make_shards(n_seq, n_dp):
    def shards(queries, neighbour_input, owner_list, block_list, enc_gain, enc_attn, kv_weight):
        full_weights = gather_weights(enc_attn, n_dp)
        me = lax.axis_index("seq")
        owners = owner_list.reshape(-1)
        indices = block_list.reshape(-1)
        refs = owners.shape[0]
        per_owner = -(-refs // n_seq)
        same = owners[:, None] == owners[None, :]
        earlier = jnp.arange(refs)[None, :] < jnp.arange(refs)[:, None]
        rank = jnp.sum(same & earlier, axis=1).astype(jnp.int32)
        asks = jnp.stack([owners, indices, rank])
        asks = jnp.broadcast_to(asks[None], (n_seq, 3, refs))
        asked = lax.all_to_all(asks, "seq", 0, 0, tiled=True)
        slots = jnp.arange(per_owner, dtype=jnp.int32)
        match = (asked[:, 0, None, :] == me) & (asked[:, 2, None, :] == slots[None, :, None])
        picks = jnp.sum(jnp.where(match, asked[:, 1, None, :], 0), axis=-1)
        sent = jnp.take(neighbour_input[0], picks.reshape(-1), axis=0, mode="clip")
        sent = sent.reshape(n_seq, per_owner, NLEN, neighbour_input.shape[-1])
        encoded = []
        for slot in range(per_owner):
            part = sent[:, slot]
            if encoded:
                part, _ = lax.optimization_barrier((part, got))
            got = lax.all_to_all(part, "seq", 0, 0, tiled=True)
            encoded.append(encode_blocks(got, enc_gain, full_weights))
        encoded = jnp.stack(encoded).reshape(per_owner * n_seq, NLEN, neighbour_input.shape[-1])
        chosen = jnp.take(encoded, rank * n_seq + owners, axis=0, mode="clip")
        chosen = chosen.reshape(refs * NLEN, neighbour_input.shape[-1])
        keys_t = jnp.einsum(
            "ef,re->fr", kv_weight[0], chosen, preferred_element_type=jnp.float32
        ).astype(jnp.bfloat16)
        values = jnp.dot(chosen, kv_weight[1], preferred_element_type=jnp.float32).astype(jnp.bfloat16)
        return cross_attend(queries[0], keys_t, values)[None]

    return shards


def solution(mesh):
    return jax.shard_map(
        make_shards(mesh.shape["seq"], mesh.shape["dp"]),
        mesh=mesh,
        in_specs=(
            P("dp", "seq", None),
            P("dp", "seq", None, None),
            P("dp", "seq", None),
            P("dp", "seq", None),
            P(),
            P(None, "dp", None),
            P(),
        ),
        out_specs=P("dp", "seq", None),
        check_vma=False,
    )
```

```python
import jax
import jax.numpy as jnp
from jax import lax
from jax.experimental import pallas as pl
from jax.experimental.pallas import tpu as pltpu
from jax.sharding import PartitionSpec as P

HEADS = 16
HEAD_DIM = 128
ENC_HEADS = 7
NLEN = 64
SPAN = 64
NEIGH = 2
NB_DEV = 4


epsilon = 1e-05


def _softmax_bf16(scores):
    highest = jnp.max(scores, axis=-1, keepdims=True)
    raised = jnp.exp(scores - highest)
    return (raised * (1.0 / jnp.sum(raised, axis=-1, keepdims=True))).astype(jnp.bfloat16)


def _encoder_kernel(order_ref, *refs):
    group = len(refs) - 8
    block_refs = refs[:group]
    gain_ref, w_ref, out_ref, q_ref, kt_ref, v_ref, mix_ref, x_ref = refs[group:]
    for b in range(group):
        x_ref[pl.ds(b * NLEN, NLEN), :] = block_refs[b][0]
    inputs = x_ref[...].astype(jnp.float32)
    spread = jnp.mean(inputs * inputs, axis=-1, keepdims=True)
    normed = (inputs * lax.rsqrt(spread + epsilon) * gain_ref[...]).astype(jnp.bfloat16)
    q_ref[...] = jnp.dot(normed, w_ref[0], preferred_element_type=jnp.float32).astype(jnp.bfloat16)
    v_ref[...] = jnp.dot(normed, w_ref[2], preferred_element_type=jnp.float32).astype(jnp.bfloat16)
    kt_ref[...] = jnp.dot(normed, w_ref[1], preferred_element_type=jnp.float32).T.astype(jnp.bfloat16)
    width = inputs.shape[-1]
    head_size = width // ENC_HEADS
    scale = head_size ** (-0.5)
    pair = 2 * NLEN
    rows_of = lax.broadcasted_iota(jnp.int32, (pair, pair), 0) // NLEN
    cols_of = lax.broadcasted_iota(jnp.int32, (pair, pair), 1) // NLEN
    same = rows_of == cols_of
    for b in range(inputs.shape[0] // pair):
        rows = pl.ds(b * pair, pair)
        for h in range(ENC_HEADS):
            cols = pl.ds(h * head_size, head_size)
            scores = jnp.dot(q_ref[rows, cols], kt_ref[cols, rows], preferred_element_type=jnp.float32) * scale
            weights = _softmax_bf16(jnp.where(same, scores, -jnp.inf))
            mix_ref[rows, cols] = jnp.dot(
                weights, v_ref[rows, cols], preferred_element_type=jnp.float32
            ).astype(jnp.bfloat16)
    output = jnp.dot(mix_ref[...], w_ref[3], preferred_element_type=jnp.float32)
    out_ref[...] = (inputs + output).astype(jnp.bfloat16)


def encode_blocks(blocks, order, gain, attention, group=8):
    count = order.shape[0]
    _, length, width = blocks.shape
    group = min(group, count)
    rows = group * length
    order = jnp.clip(order, 0, blocks.shape[0] - 1).astype(jnp.int32)

    def block_spec(j):
        return pl.BlockSpec((1, length, width), lambda i, order_ref: (order_ref[i * group + j], 0, 0))

    grid_spec = pltpu.PrefetchScalarGridSpec(
        num_scalar_prefetch=1,
        grid=(count // group,),
        in_specs=[block_spec(j) for j in range(group)]
        + [
            pl.BlockSpec((1, width), lambda i, order_ref: (0, 0)),
            pl.BlockSpec(attention.shape, lambda i, order_ref: (0, 0, 0)),
        ],
        out_specs=pl.BlockSpec((rows, width), lambda i, order_ref: (i, 0)),
        scratch_shapes=[
            pltpu.VMEM((rows, width), jnp.bfloat16),
            pltpu.VMEM((width, rows), jnp.bfloat16),
            pltpu.VMEM((rows, width), jnp.bfloat16),
            pltpu.VMEM((rows, width), jnp.bfloat16),
            pltpu.VMEM((rows, width), blocks.dtype),
        ],
    )
    return pl.pallas_call(
        _encoder_kernel,
        out_shape=jax.ShapeDtypeStruct((count * length, width), jnp.bfloat16),
        grid_spec=grid_spec,
    )(order, *([blocks] * group), gain.reshape(1, width), attention)


def _cross_kernel(q_ref, kt_ref, v_ref, out_ref):
    scale = HEAD_DIM ** (-0.5)
    memory = NEIGH * NLEN
    for s in range(q_ref.shape[0] // SPAN):
        rq = pl.ds(s * SPAN, SPAN)
        rk = pl.ds(s * memory, memory)
        for h in range(q_ref.shape[-1] // HEAD_DIM):
            cols = pl.ds(h * HEAD_DIM, HEAD_DIM)
            scores = jnp.dot(q_ref[rq, cols], kt_ref[cols, rk], preferred_element_type=jnp.float32) * scale
            weights = _softmax_bf16(scores)
            out_ref[rq, cols] = jnp.dot(
                weights, v_ref[rk, cols], preferred_element_type=jnp.float32
            ).astype(jnp.bfloat16)


def cross_attend(queries, keys_t, values, group=4):
    length, width = queries.shape
    memory = NEIGH * NLEN
    group = min(group, length // SPAN)
    return pl.pallas_call(
        _cross_kernel,
        out_shape=jax.ShapeDtypeStruct(queries.shape, jnp.bfloat16),
        grid=(length // (SPAN * group),),
        in_specs=[
            pl.BlockSpec((SPAN * group, width), lambda c: (c, 0)),
            pl.BlockSpec((width, memory * group), lambda c: (0, c)),
            pl.BlockSpec((memory * group, width), lambda c: (c, 0)),
        ],
        out_specs=pl.BlockSpec((SPAN * group, width), lambda c: (c, 0)),
    )(queries, keys_t, values)


def gather_weights(shard, n_dp):
    n_x = n_dp // 2
    place = lax.axis_index("dp")
    x, core = place // 2, place % 2
    pieces = [(shard, place)]
    for shift in range(1, n_x):
        ring = [(src, ((src // 2 + shift) % n_x) * 2 + src % 2) for src in range(n_dp)]
        pieces.append((lax.ppermute(shard, "dp", ring), ((x - shift) % n_x) * 2 + core))
    swap = [(src, src ^ 1) for src in range(n_dp)]
    pieces += [(lax.ppermute(piece, "dp", swap), owner ^ 1) for piece, owner in pieces]
    count, rows, width = shard.shape
    full = jnp.zeros((count, n_dp * rows, width), shard.dtype)
    for piece, owner in pieces:
        full = lax.dynamic_update_slice(full, piece, (0, owner * rows, 0))
    return full


def make_shards(n_seq, n_dp):
    def shards(queries, neighbour_input, owner_list, block_list, enc_gain, enc_attn, kv_weight):
        full_weights = gather_weights(enc_attn, n_dp)
        me = lax.axis_index("seq")
        owners = owner_list.reshape(-1)
        indices = block_list.reshape(-1)
        refs = owners.shape[0]
        per_owner = -(-refs // n_seq)
        same = owners[:, None] == owners[None, :]
        earlier = jnp.arange(refs)[None, :] < jnp.arange(refs)[:, None]
        rank = jnp.sum(same & earlier, axis=1).astype(jnp.int32)
        asks = jnp.stack([owners, indices, rank])
        asks = jnp.broadcast_to(asks[None], (n_seq, 3, refs))
        asked = lax.all_to_all(asks, "seq", 0, 0, tiled=True)
        slots = jnp.arange(per_owner, dtype=jnp.int32)
        match = (asked[:, 0, None, :] == me) & (asked[:, 2, None, :] == slots[None, :, None])
        picks = jnp.sum(jnp.where(match, asked[:, 1, None, :], 0), axis=-1)
        sent = jnp.take(neighbour_input[0], picks.reshape(-1), axis=0, mode="clip")
        sent = sent.reshape(n_seq, per_owner, NLEN, neighbour_input.shape[-1])
        got = lax.all_to_all(sent, "seq", 0, 0, tiled=True)
        got = got.reshape(n_seq * per_owner, NLEN, neighbour_input.shape[-1])
        chosen = encode_blocks(got, owners * per_owner + rank, enc_gain, full_weights)
        keys_t = jnp.einsum(
            "ef,re->fr", kv_weight[0], chosen, preferred_element_type=jnp.float32
        ).astype(jnp.bfloat16)
        values = jnp.dot(chosen, kv_weight[1], preferred_element_type=jnp.float32).astype(jnp.bfloat16)
        return cross_attend(queries[0], keys_t, values)[None]

    return shards


def solution(mesh):
    return jax.shard_map(
        make_shards(mesh.shape["seq"], mesh.shape["dp"]),
        mesh=mesh,
        in_specs=(
            P("dp", "seq", None),
            P("dp", "seq", None, None),
            P("dp", "seq", None),
            P("dp", "seq", None),
            P(),
            P(None, "dp", None),
            P(),
        ),
        out_specs=P("dp", "seq", None),
        check_vma=False,
    )
```

```python
import jax
import jax.numpy as jnp
from jax import lax
from jax.experimental import pallas as pl
from jax.experimental.pallas import tpu as pltpu
from jax.sharding import PartitionSpec as P

HEADS = 16
HEAD_DIM = 128
ENC_HEADS = 7
NLEN = 64
SPAN = 64
NEIGH = 2
NB_DEV = 4


epsilon = 1e-05


def _softmax_bf16(scores):
    highest = jnp.max(scores, axis=-1, keepdims=True)
    raised = jnp.exp(scores - highest)
    return (raised * (1.0 / jnp.sum(raised, axis=-1, keepdims=True))).astype(jnp.bfloat16)


def _encoder_kernel(x_ref, gain_ref, w_ref, out_ref, q_ref, kt_ref, v_ref, mix_ref):
    inputs = x_ref[...].astype(jnp.float32)
    spread = jnp.mean(inputs * inputs, axis=-1, keepdims=True)
    normed = (inputs * lax.rsqrt(spread + epsilon) * gain_ref[...]).astype(jnp.bfloat16)
    q_ref[...] = jnp.dot(normed, w_ref[0], preferred_element_type=jnp.float32).astype(jnp.bfloat16)
    v_ref[...] = jnp.dot(normed, w_ref[2], preferred_element_type=jnp.float32).astype(jnp.bfloat16)
    kt_ref[...] = jnp.dot(normed, w_ref[1], preferred_element_type=jnp.float32).T.astype(jnp.bfloat16)
    width = inputs.shape[-1]
    head_size = width // ENC_HEADS
    scale = head_size ** (-0.5)
    pair = 2 * NLEN
    rows_of = lax.broadcasted_iota(jnp.int32, (pair, pair), 0) // NLEN
    cols_of = lax.broadcasted_iota(jnp.int32, (pair, pair), 1) // NLEN
    same = rows_of == cols_of
    for b in range(inputs.shape[0] // pair):
        rows = pl.ds(b * pair, pair)
        for h in range(ENC_HEADS):
            cols = pl.ds(h * head_size, head_size)
            scores = jnp.dot(q_ref[rows, cols], kt_ref[cols, rows], preferred_element_type=jnp.float32) * scale
            weights = _softmax_bf16(jnp.where(same, scores, -jnp.inf))
            mix_ref[rows, cols] = jnp.dot(
                weights, v_ref[rows, cols], preferred_element_type=jnp.float32
            ).astype(jnp.bfloat16)
    output = jnp.dot(mix_ref[...], w_ref[3], preferred_element_type=jnp.float32)
    out_ref[...] = (inputs + output).astype(jnp.bfloat16)


def encode_blocks(blocks, gain, attention, group=8):
    count, length, width = blocks.shape
    group = min(group, count)
    rows = group * length
    flat = blocks.reshape(count * length, width)
    return pl.pallas_call(
        _encoder_kernel,
        out_shape=jax.ShapeDtypeStruct(flat.shape, jnp.bfloat16),
        grid=(count // group,),
        in_specs=[
            pl.BlockSpec((rows, width), lambda i: (i, 0)),
            pl.BlockSpec((1, width), lambda i: (0, 0)),
            pl.BlockSpec(attention.shape, lambda i: (0, 0, 0)),
        ],
        out_specs=pl.BlockSpec((rows, width), lambda i: (i, 0)),
        scratch_shapes=[
            pltpu.VMEM((rows, width), jnp.bfloat16),
            pltpu.VMEM((width, rows), jnp.bfloat16),
            pltpu.VMEM((rows, width), jnp.bfloat16),
            pltpu.VMEM((rows, width), jnp.bfloat16),
        ],
    )(flat, gain.reshape(1, width), attention)


def _cross_kernel(qt_ref, kv_ref, out_ref):
    scale = HEAD_DIM ** (-0.5)
    spans, memory = 2 * SPAN, 2 * NEIGH * NLEN
    key_of = lax.broadcasted_iota(jnp.int32, (memory, spans), 0) // (NEIGH * NLEN)
    query_of = lax.broadcasted_iota(jnp.int32, (memory, spans), 1) // SPAN
    same = key_of == query_of
    half = kv_ref.shape[-1] // 2
    for p in range(qt_ref.shape[-1] // spans):
        rq = pl.ds(p * spans, spans)
        rk = pl.ds(p * memory, memory)
        for h in range(half // HEAD_DIM):
            cols = pl.ds(h * HEAD_DIM, HEAD_DIM)
            scores = jnp.dot(kv_ref[rk, cols], qt_ref[cols, rq], preferred_element_type=jnp.float32) * scale
            scores = jnp.where(same, scores, -jnp.inf)
            highest = jnp.max(scores, axis=0, keepdims=True)
            raised = jnp.exp(scores - highest)
            weights = (raised * (1.0 / jnp.sum(raised, axis=0, keepdims=True))).astype(jnp.bfloat16)
            out_ref[rq, cols] = lax.dot_general(
                weights, kv_ref[rk, pl.ds(half + h * HEAD_DIM, HEAD_DIM)],
                (((0,), (0,)), ((), ())), preferred_element_type=jnp.float32,
            ).astype(jnp.bfloat16)


def cross_attend(queries_t, keys_values, group=2):
    width, length = queries_t.shape
    spans = 2 * SPAN
    memory = 2 * NEIGH * NLEN
    group = min(group, length // spans)
    return pl.pallas_call(
        _cross_kernel,
        out_shape=jax.ShapeDtypeStruct((length, width), jnp.bfloat16),
        grid=(length // (spans * group),),
        in_specs=[
            pl.BlockSpec((width, spans * group), lambda c: (0, c)),
            pl.BlockSpec((memory * group, 2 * width), lambda c: (c, 0)),
        ],
        out_specs=pl.BlockSpec((spans * group, width), lambda c: (c, 0)),
    )(queries_t, keys_values)


def gather_weights(shard, n_dp):
    n_x = n_dp // 2
    place = lax.axis_index("dp")
    x, core = place // 2, place % 2
    pieces = [(shard, place)]
    for shift in range(1, n_x):
        ring = [(src, ((src // 2 + shift) % n_x) * 2 + src % 2) for src in range(n_dp)]
        pieces.append((lax.ppermute(shard, "dp", ring), ((x - shift) % n_x) * 2 + core))
    swap = [(src, src ^ 1) for src in range(n_dp)]
    pieces += [(lax.ppermute(piece, "dp", swap), owner ^ 1) for piece, owner in pieces]
    count, rows, width = shard.shape
    full = jnp.zeros((count, n_dp * rows, width), shard.dtype)
    for piece, owner in pieces:
        full = lax.dynamic_update_slice(full, piece, (0, owner * rows, 0))
    return full


def make_shards(n_seq, n_dp):
    def shards(queries, neighbour_input, owner_list, block_list, enc_gain, enc_attn, kv_weight):
        full_weights = gather_weights(enc_attn, n_dp)
        me = lax.axis_index("seq")
        owners = owner_list.reshape(-1)
        indices = block_list.reshape(-1)
        refs = owners.shape[0]
        per_owner = -(-refs // n_seq)
        same = owners[:, None] == owners[None, :]
        earlier = jnp.arange(refs)[None, :] < jnp.arange(refs)[:, None]
        rank = jnp.sum(same & earlier, axis=1).astype(jnp.int32)
        asks = jnp.stack([owners, indices, rank])
        asks = jnp.broadcast_to(asks[None], (n_seq, 3, refs))
        asked = lax.all_to_all(asks, "seq", 0, 0, tiled=True)
        slots = jnp.arange(per_owner, dtype=jnp.int32)
        match = (asked[:, 0, None, :] == me) & (asked[:, 2, None, :] == slots[None, :, None])
        picks = jnp.sum(jnp.where(match, asked[:, 1, None, :], 0), axis=-1)
        sent = jnp.take(neighbour_input[0], picks.reshape(-1), axis=0, mode="clip")
        sent = sent.reshape(n_seq, per_owner, NLEN, neighbour_input.shape[-1])
        got = lax.all_to_all(sent, "seq", 0, 0, tiled=True)
        got = got.reshape(n_seq * per_owner, NLEN, neighbour_input.shape[-1])
        chosen_raw = jnp.take(got, owners * per_owner + rank, axis=0, mode="clip")
        chosen = encode_blocks(chosen_raw, enc_gain, full_weights)
        both = jnp.concatenate([kv_weight[0], kv_weight[1]], axis=1)
        keys_values = jnp.dot(chosen, both, preferred_element_type=jnp.float32).astype(jnp.bfloat16)
        return cross_attend(queries[0].T, keys_values)[None]

    return shards


def solution(mesh):
    return jax.shard_map(
        make_shards(mesh.shape["seq"], mesh.shape["dp"]),
        mesh=mesh,
        in_specs=(
            P("dp", "seq", None),
            P("dp", "seq", None, None),
            P("dp", "seq", None),
            P("dp", "seq", None),
            P(),
            P(None, "dp", None),
            P(),
        ),
        out_specs=P("dp", "seq", None),
        check_vma=False,
    )
```

```python
import jax
import jax.numpy as jnp
from jax import lax
from jax.experimental import pallas as pl
from jax.experimental.pallas import tpu as pltpu
from jax.sharding import PartitionSpec as P

HEADS = 16
HEAD_DIM = 128
ENC_HEADS = 7
NLEN = 64
SPAN = 64
NEIGH = 2
NB_DEV = 4


epsilon = 1e-05


def _softmax_bf16(scores):
    highest = jnp.max(scores, axis=-1, keepdims=True)
    raised = jnp.exp(scores - highest)
    return (raised * (1.0 / jnp.sum(raised, axis=-1, keepdims=True))).astype(jnp.bfloat16)


def _encoder_kernel(x_ref, gain_ref, w_ref, out_ref, q_ref, kt_ref, v_ref, mix_ref):
    inputs = x_ref[...].astype(jnp.float32)
    spread = jnp.mean(inputs * inputs, axis=-1, keepdims=True)
    normed = (inputs * lax.rsqrt(spread + epsilon) * gain_ref[...]).astype(jnp.bfloat16)
    q_ref[...] = jnp.dot(normed, w_ref[0], preferred_element_type=jnp.float32).astype(jnp.bfloat16)
    v_ref[...] = jnp.dot(normed, w_ref[2], preferred_element_type=jnp.float32).astype(jnp.bfloat16)
    kt_ref[...] = jnp.dot(normed, w_ref[1], preferred_element_type=jnp.float32).T.astype(jnp.bfloat16)
    width = inputs.shape[-1]
    head_size = width // ENC_HEADS
    scale = head_size ** (-0.5)
    pair = 2 * NLEN
    rows_of = lax.broadcasted_iota(jnp.int32, (pair, pair), 0) // NLEN
    cols_of = lax.broadcasted_iota(jnp.int32, (pair, pair), 1) // NLEN
    same = rows_of == cols_of
    for b in range(inputs.shape[0] // pair):
        rows = pl.ds(b * pair, pair)
        for h in range(ENC_HEADS):
            cols = pl.ds(h * head_size, head_size)
            scores = jnp.dot(q_ref[rows, cols], kt_ref[cols, rows], preferred_element_type=jnp.float32) * scale
            weights = _softmax_bf16(jnp.where(same, scores, -jnp.inf))
            mix_ref[rows, cols] = jnp.dot(
                weights, v_ref[rows, cols], preferred_element_type=jnp.float32
            ).astype(jnp.bfloat16)
    output = jnp.dot(mix_ref[...], w_ref[3], preferred_element_type=jnp.float32)
    out_ref[...] = (inputs + output).astype(jnp.bfloat16)


def encode_blocks(blocks, gain, attention, group=16):
    count, length, width = blocks.shape
    group = min(group, count)
    rows = group * length
    flat = blocks.reshape(count * length, width)
    return pl.pallas_call(
        _encoder_kernel,
        out_shape=jax.ShapeDtypeStruct(flat.shape, jnp.bfloat16),
        grid=(count // group,),
        in_specs=[
            pl.BlockSpec((rows, width), lambda i: (i, 0)),
            pl.BlockSpec((1, width), lambda i: (0, 0)),
            pl.BlockSpec(attention.shape, lambda i: (0, 0, 0)),
        ],
        out_specs=pl.BlockSpec((rows, width), lambda i: (i, 0)),
        scratch_shapes=[
            pltpu.VMEM((rows, width), jnp.bfloat16),
            pltpu.VMEM((width, rows), jnp.bfloat16),
            pltpu.VMEM((rows, width), jnp.bfloat16),
            pltpu.VMEM((rows, width), jnp.bfloat16),
        ],
    )(flat, gain.reshape(1, width), attention)


def _cross_kernel(q_ref, kt_ref, v_ref, out_ref):
    scale = HEAD_DIM ** (-0.5)
    memory = NEIGH * NLEN
    for s in range(q_ref.shape[0] // SPAN):
        rq = pl.ds(s * SPAN, SPAN)
        rk = pl.ds(s * memory, memory)
        for h in range(q_ref.shape[-1] // HEAD_DIM):
            cols = pl.ds(h * HEAD_DIM, HEAD_DIM)
            scores = jnp.dot(q_ref[rq, cols], kt_ref[cols, rk], preferred_element_type=jnp.float32) * scale
            weights = _softmax_bf16(scores)
            out_ref[rq, cols] = jnp.dot(
                weights, v_ref[rk, cols], preferred_element_type=jnp.float32
            ).astype(jnp.bfloat16)


def cross_attend(queries, keys_t, values, group=8):
    length, width = queries.shape
    memory = NEIGH * NLEN
    group = min(group, length // SPAN)
    return pl.pallas_call(
        _cross_kernel,
        out_shape=jax.ShapeDtypeStruct(queries.shape, jnp.bfloat16),
        grid=(length // (SPAN * group),),
        in_specs=[
            pl.BlockSpec((SPAN * group, width), lambda c: (c, 0)),
            pl.BlockSpec((width, memory * group), lambda c: (0, c)),
            pl.BlockSpec((memory * group, width), lambda c: (c, 0)),
        ],
        out_specs=pl.BlockSpec((SPAN * group, width), lambda c: (c, 0)),
    )(queries, keys_t, values)


def gather_weights(shard, n_dp):
    n_x = n_dp // 2
    place = lax.axis_index("dp")
    x, core = place // 2, place % 2
    pieces = [(shard, place)]
    for shift in range(1, n_x):
        ring = [(src, ((src // 2 + shift) % n_x) * 2 + src % 2) for src in range(n_dp)]
        pieces.append((lax.ppermute(shard, "dp", ring), ((x - shift) % n_x) * 2 + core))
    swap = [(src, src ^ 1) for src in range(n_dp)]
    pieces += [(lax.ppermute(piece, "dp", swap), owner ^ 1) for piece, owner in pieces]
    count, rows, width = shard.shape
    full = jnp.zeros((count, n_dp * rows, width), shard.dtype)
    for piece, owner in pieces:
        full = lax.dynamic_update_slice(full, piece, (0, owner * rows, 0))
    return full


def make_shards(n_seq, n_dp):
    def shards(queries, neighbour_input, owner_list, block_list, enc_gain, enc_attn, kv_weight):
        full_weights = gather_weights(enc_attn, n_dp)
        me = lax.axis_index("seq")
        owners = owner_list.reshape(-1)
        indices = block_list.reshape(-1)
        refs = owners.shape[0]
        per_owner = -(-refs // n_seq)
        same = owners[:, None] == owners[None, :]
        earlier = jnp.arange(refs)[None, :] < jnp.arange(refs)[:, None]
        rank = jnp.sum(same & earlier, axis=1).astype(jnp.int32)
        asks = jnp.stack([owners, indices, rank])
        asks = jnp.broadcast_to(asks[None], (n_seq, 3, refs))
        asked = lax.all_to_all(asks, "seq", 0, 0, tiled=True)
        slots = jnp.arange(per_owner, dtype=jnp.int32)
        match = (asked[:, 0, None, :] == me) & (asked[:, 2, None, :] == slots[None, :, None])
        picks = jnp.sum(jnp.where(match, asked[:, 1, None, :], 0), axis=-1)
        sent = jnp.take(neighbour_input[0], picks.reshape(-1), axis=0, mode="clip")
        sent = sent.reshape(n_seq, per_owner, NLEN, neighbour_input.shape[-1])
        got = lax.all_to_all(sent, "seq", 0, 0, tiled=True)
        got = got.reshape(n_seq * per_owner, NLEN, neighbour_input.shape[-1])
        chosen_raw = jnp.take(got, owners * per_owner + rank, axis=0, mode="clip")
        chosen = encode_blocks(chosen_raw, enc_gain, full_weights)
        keys_t = jnp.einsum(
            "ef,re->fr", kv_weight[0], chosen, preferred_element_type=jnp.float32
        ).astype(jnp.bfloat16)
        values = jnp.dot(chosen, kv_weight[1], preferred_element_type=jnp.float32).astype(jnp.bfloat16)
        return cross_attend(queries[0], keys_t, values)[None]

    return shards


def solution(mesh):
    return jax.shard_map(
        make_shards(mesh.shape["seq"], mesh.shape["dp"]),
        mesh=mesh,
        in_specs=(
            P("dp", "seq", None),
            P("dp", "seq", None, None),
            P("dp", "seq", None),
            P("dp", "seq", None),
            P(),
            P(None, "dp", None),
            P(),
        ),
        out_specs=P("dp", "seq", None),
        check_vma=False,
    )
```

```python
import jax
import jax.numpy as jnp
from jax import lax
from jax.experimental import pallas as pl
from jax.experimental.pallas import tpu as pltpu
from jax.sharding import PartitionSpec as P

HEADS = 16
HEAD_DIM = 128
ENC_HEADS = 7
NLEN = 64
SPAN = 64
NEIGH = 2
NB_DEV = 4


epsilon = 1e-05


def _softmax_bf16(scores):
    highest = jnp.max(scores, axis=-1, keepdims=True)
    raised = jnp.exp(scores - highest)
    return (raised * (1.0 / jnp.sum(raised, axis=-1, keepdims=True))).astype(jnp.bfloat16)


def _encoder_kernel(x_ref, gain_ref, w_ref, out_ref, q_ref, kt_ref, v_ref, mix_ref):
    inputs = x_ref[...].astype(jnp.float32)
    spread = jnp.mean(inputs * inputs, axis=-1, keepdims=True)
    normed = (inputs * lax.rsqrt(spread + epsilon) * gain_ref[...]).astype(jnp.bfloat16)
    q_ref[...] = jnp.dot(normed, w_ref[0], preferred_element_type=jnp.float32).astype(jnp.bfloat16)
    v_ref[...] = jnp.dot(normed, w_ref[2], preferred_element_type=jnp.float32).astype(jnp.bfloat16)
    kt_ref[...] = jnp.dot(normed, w_ref[1], preferred_element_type=jnp.float32).T.astype(jnp.bfloat16)
    width = inputs.shape[-1]
    head_size = width // ENC_HEADS
    scale = head_size ** (-0.5)
    pair = 2 * NLEN
    rows_of = lax.broadcasted_iota(jnp.int32, (pair, pair), 0) // NLEN
    cols_of = lax.broadcasted_iota(jnp.int32, (pair, pair), 1) // NLEN
    same = rows_of == cols_of
    for b in range(inputs.shape[0] // pair):
        rows = pl.ds(b * pair, pair)
        for h in range(ENC_HEADS):
            cols = pl.ds(h * head_size, head_size)
            scores = jnp.dot(q_ref[rows, cols], kt_ref[cols, rows], preferred_element_type=jnp.float32) * scale
            weights = _softmax_bf16(jnp.where(same, scores, -jnp.inf))
            mix_ref[rows, cols] = jnp.dot(
                weights, v_ref[rows, cols], preferred_element_type=jnp.float32
            ).astype(jnp.bfloat16)
    output = jnp.dot(mix_ref[...], w_ref[3], preferred_element_type=jnp.float32)
    out_ref[...] = (inputs + output).astype(jnp.bfloat16)


def encode_blocks(blocks, gain, attention, group=8):
    count, length, width = blocks.shape
    group = min(group, count)
    rows = group * length
    flat = blocks.reshape(count * length, width)
    return pl.pallas_call(
        _encoder_kernel,
        out_shape=jax.ShapeDtypeStruct(flat.shape, jnp.bfloat16),
        grid=(count // group,),
        in_specs=[
            pl.BlockSpec((rows, width), lambda i: (i, 0)),
            pl.BlockSpec((1, width), lambda i: (0, 0)),
            pl.BlockSpec(attention.shape, lambda i: (0, 0, 0)),
        ],
        out_specs=pl.BlockSpec((rows, width), lambda i: (i, 0)),
        scratch_shapes=[
            pltpu.VMEM((rows, width), jnp.bfloat16),
            pltpu.VMEM((width, rows), jnp.bfloat16),
            pltpu.VMEM((rows, width), jnp.bfloat16),
            pltpu.VMEM((rows, width), jnp.bfloat16),
        ],
    )(flat, gain.reshape(1, width), attention)


def _cross_kernel(q_ref, kt_ref, v_ref, out_ref):
    scale = HEAD_DIM ** (-0.5)
    memory = NEIGH * NLEN
    for s in range(q_ref.shape[0] // SPAN):
        rq = pl.ds(s * SPAN, SPAN)
        rk = pl.ds(s * memory, memory)
        for h in range(q_ref.shape[-1] // HEAD_DIM):
            cols = pl.ds(h * HEAD_DIM, HEAD_DIM)
            scores = jnp.dot(q_ref[rq, cols], kt_ref[cols, rk], preferred_element_type=jnp.float32) * scale
            weights = _softmax_bf16(scores)
            out_ref[rq, cols] = jnp.dot(
                weights, v_ref[rk, cols], preferred_element_type=jnp.float32
            ).astype(jnp.bfloat16)


def cross_attend(queries, keys_t, values, group=4):
    length, width = queries.shape
    memory = NEIGH * NLEN
    group = min(group, length // SPAN)
    return pl.pallas_call(
        _cross_kernel,
        out_shape=jax.ShapeDtypeStruct(queries.shape, jnp.bfloat16),
        grid=(length // (SPAN * group),),
        in_specs=[
            pl.BlockSpec((SPAN * group, width), lambda c: (c, 0)),
            pl.BlockSpec((width, memory * group), lambda c: (0, c)),
            pl.BlockSpec((memory * group, width), lambda c: (c, 0)),
        ],
        out_specs=pl.BlockSpec((SPAN * group, width), lambda c: (c, 0)),
    )(queries, keys_t, values)


def gather_weights(shard, n_dp):
    n_x = n_dp // 2
    place = lax.axis_index("dp")
    x, core = place // 2, place % 2
    pieces = [(shard, place)]
    for shift in range(1, n_x):
        ring = [(src, ((src // 2 + shift) % n_x) * 2 + src % 2) for src in range(n_dp)]
        pieces.append((lax.ppermute(shard, "dp", ring), ((x - shift) % n_x) * 2 + core))
    swap = [(src, src ^ 1) for src in range(n_dp)]
    pieces += [(lax.ppermute(piece, "dp", swap), owner ^ 1) for piece, owner in pieces]
    count, rows, width = shard.shape
    full = jnp.zeros((count, n_dp * rows, width), shard.dtype)
    for piece, owner in pieces:
        full = lax.dynamic_update_slice(full, piece, (0, owner * rows, 0))
    return full


def make_shards(n_seq, n_dp):
    def shards(queries, neighbour_input, owner_list, block_list, enc_gain, enc_attn, kv_weight):
        full_weights = gather_weights(enc_attn, n_dp)
        me = lax.axis_index("seq")
        owners = owner_list.reshape(-1)
        indices = block_list.reshape(-1)
        refs = owners.shape[0]
        per_owner = -(-refs // n_seq)
        asks = jnp.stack([owners, indices])
        asks = jnp.broadcast_to(asks[None], (n_seq, 2, refs))
        asked = lax.all_to_all(asks, "seq", 0, 0, tiled=True)
        earlier = jnp.arange(refs)[None, :] < jnp.arange(refs)[:, None]

        def rank_of(names):
            return jnp.sum((names[..., :, None] == names[..., None, :]) & earlier, axis=-1)

        rank = rank_of(owners).astype(jnp.int32)
        asked_rank = rank_of(asked[:, 0])
        slots = jnp.arange(per_owner, dtype=jnp.int32)
        match = (asked[:, 0, None, :] == me) & (asked_rank[:, None, :] == slots[None, :, None])
        picks = jnp.sum(jnp.where(match, asked[:, 1, None, :], 0), axis=-1)
        sent = jnp.take(neighbour_input[0], picks.reshape(-1), axis=0, mode="clip")
        sent = sent.reshape(n_seq, per_owner, NLEN, neighbour_input.shape[-1])
        got = lax.all_to_all(sent, "seq", 0, 0, tiled=True)
        got = got.reshape(n_seq * per_owner, NLEN, neighbour_input.shape[-1])
        chosen_raw = jnp.take(got, owners * per_owner + rank, axis=0, mode="clip")
        chosen = encode_blocks(chosen_raw, enc_gain, full_weights)
        keys_t = jnp.einsum(
            "ef,re->fr", kv_weight[0], chosen, preferred_element_type=jnp.float32
        ).astype(jnp.bfloat16)
        values = jnp.dot(chosen, kv_weight[1], preferred_element_type=jnp.float32).astype(jnp.bfloat16)
        return cross_attend(queries[0], keys_t, values)[None]

    return shards


def solution(mesh):
    return jax.shard_map(
        make_shards(mesh.shape["seq"], mesh.shape["dp"]),
        mesh=mesh,
        in_specs=(
            P("dp", "seq", None),
            P("dp", "seq", None, None),
            P("dp", "seq", None),
            P("dp", "seq", None),
            P(),
            P(None, "dp", None),
            P(),
        ),
        out_specs=P("dp", "seq", None),
        check_vma=False,
    )
```

```python
import jax
import jax.numpy as jnp
from jax import lax
from jax.experimental import pallas as pl
from jax.experimental.pallas import tpu as pltpu
from jax.sharding import PartitionSpec as P

HEADS = 16
HEAD_DIM = 128
ENC_HEADS = 7
NLEN = 64
SPAN = 64
NEIGH = 2
NB_DEV = 4


epsilon = 1e-05


def _softmax_bf16(scores):
    highest = jnp.max(scores, axis=-1, keepdims=True)
    raised = jnp.exp(scores - highest)
    return (raised * (1.0 / jnp.sum(raised, axis=-1, keepdims=True))).astype(jnp.bfloat16)


def _encoder_kernel(x_ref, gain_ref, w_hbm, out_ref, w_ref, sems, q_ref, kt_ref, v_ref, mix_ref):
    first = pl.program_id(0) == 0
    copies = [pltpu.make_async_copy(w_hbm.at[p], w_ref.at[p], sems.at[p]) for p in range(4)]

    @pl.when(first)
    def _():
        for copy in copies:
            copy.start()

    def ready(p):
        @pl.when(first)
        def _():
            copies[p].wait()

    inputs = x_ref[...].astype(jnp.float32)
    spread = jnp.mean(inputs * inputs, axis=-1, keepdims=True)
    normed = (inputs * lax.rsqrt(spread + epsilon) * gain_ref[...]).astype(jnp.bfloat16)
    ready(0)
    q_ref[...] = jnp.dot(normed, w_ref[0], preferred_element_type=jnp.float32).astype(jnp.bfloat16)
    ready(1)
    kt_ref[...] = jnp.dot(normed, w_ref[1], preferred_element_type=jnp.float32).T.astype(jnp.bfloat16)
    ready(2)
    v_ref[...] = jnp.dot(normed, w_ref[2], preferred_element_type=jnp.float32).astype(jnp.bfloat16)
    width = inputs.shape[-1]
    head_size = width // ENC_HEADS
    scale = head_size ** (-0.5)
    pair = 2 * NLEN
    rows_of = lax.broadcasted_iota(jnp.int32, (pair, pair), 0) // NLEN
    cols_of = lax.broadcasted_iota(jnp.int32, (pair, pair), 1) // NLEN
    same = rows_of == cols_of
    for b in range(inputs.shape[0] // pair):
        rows = pl.ds(b * pair, pair)
        for h in range(ENC_HEADS):
            cols = pl.ds(h * head_size, head_size)
            scores = jnp.dot(q_ref[rows, cols], kt_ref[cols, rows], preferred_element_type=jnp.float32) * scale
            weights = _softmax_bf16(jnp.where(same, scores, -jnp.inf))
            mix_ref[rows, cols] = jnp.dot(
                weights, v_ref[rows, cols], preferred_element_type=jnp.float32
            ).astype(jnp.bfloat16)
    ready(3)
    output = jnp.dot(mix_ref[...], w_ref[3], preferred_element_type=jnp.float32)
    out_ref[...] = (inputs + output).astype(jnp.bfloat16)


def encode_blocks(blocks, gain, attention, group=8):
    count, length, width = blocks.shape
    group = min(group, count)
    rows = group * length
    flat = blocks.reshape(count * length, width)
    return pl.pallas_call(
        _encoder_kernel,
        out_shape=jax.ShapeDtypeStruct(flat.shape, jnp.bfloat16),
        grid=(count // group,),
        in_specs=[
            pl.BlockSpec((rows, width), lambda i: (i, 0)),
            pl.BlockSpec((1, width), lambda i: (0, 0)),
            pl.BlockSpec(memory_space=pl.ANY),
        ],
        out_specs=pl.BlockSpec((rows, width), lambda i: (i, 0)),
        scratch_shapes=[
            pltpu.VMEM(attention.shape, attention.dtype),
            pltpu.SemaphoreType.DMA((4,)),
            pltpu.VMEM((rows, width), jnp.bfloat16),
            pltpu.VMEM((width, rows), jnp.bfloat16),
            pltpu.VMEM((rows, width), jnp.bfloat16),
            pltpu.VMEM((rows, width), jnp.bfloat16),
        ],
        compiler_params=pltpu.CompilerParams(dimension_semantics=("arbitrary",)),
    )(flat, gain.reshape(1, width), attention)


def _cross_kernel(q_ref, kt_ref, v_ref, out_ref):
    scale = HEAD_DIM ** (-0.5)
    memory = NEIGH * NLEN
    for s in range(q_ref.shape[0] // SPAN):
        rq = pl.ds(s * SPAN, SPAN)
        rk = pl.ds(s * memory, memory)
        for h in range(q_ref.shape[-1] // HEAD_DIM):
            cols = pl.ds(h * HEAD_DIM, HEAD_DIM)
            scores = jnp.dot(q_ref[rq, cols], kt_ref[cols, rk], preferred_element_type=jnp.float32) * scale
            weights = _softmax_bf16(scores)
            out_ref[rq, cols] = jnp.dot(
                weights, v_ref[rk, cols], preferred_element_type=jnp.float32
            ).astype(jnp.bfloat16)


def cross_attend(queries, keys_t, values, group=4):
    length, width = queries.shape
    memory = NEIGH * NLEN
    group = min(group, length // SPAN)
    return pl.pallas_call(
        _cross_kernel,
        out_shape=jax.ShapeDtypeStruct(queries.shape, jnp.bfloat16),
        grid=(length // (SPAN * group),),
        in_specs=[
            pl.BlockSpec((SPAN * group, width), lambda c: (c, 0)),
            pl.BlockSpec((width, memory * group), lambda c: (0, c)),
            pl.BlockSpec((memory * group, width), lambda c: (c, 0)),
        ],
        out_specs=pl.BlockSpec((SPAN * group, width), lambda c: (c, 0)),
    )(queries, keys_t, values)


def gather_weights(shard, n_dp):
    n_x = n_dp // 2
    place = lax.axis_index("dp")
    x, core = place // 2, place % 2
    pieces = [(shard, place)]
    for shift in range(1, n_x):
        ring = [(src, ((src // 2 + shift) % n_x) * 2 + src % 2) for src in range(n_dp)]
        pieces.append((lax.ppermute(shard, "dp", ring), ((x - shift) % n_x) * 2 + core))
    swap = [(src, src ^ 1) for src in range(n_dp)]
    pieces += [(lax.ppermute(piece, "dp", swap), owner ^ 1) for piece, owner in pieces]
    count, rows, width = shard.shape
    full = jnp.zeros((count, n_dp * rows, width), shard.dtype)
    for piece, owner in pieces:
        full = lax.dynamic_update_slice(full, piece, (0, owner * rows, 0))
    return full


def make_shards(n_seq, n_dp):
    def shards(queries, neighbour_input, owner_list, block_list, enc_gain, enc_attn, kv_weight):
        full_weights = gather_weights(enc_attn, n_dp)
        me = lax.axis_index("seq")
        owners = owner_list.reshape(-1)
        indices = block_list.reshape(-1)
        refs = owners.shape[0]
        per_owner = -(-refs // n_seq)
        same = owners[:, None] == owners[None, :]
        earlier = jnp.arange(refs)[None, :] < jnp.arange(refs)[:, None]
        rank = jnp.sum(same & earlier, axis=1).astype(jnp.int32)
        asks = jnp.stack([owners, indices, rank])
        asks = jnp.broadcast_to(asks[None], (n_seq, 3, refs))
        asked = lax.all_to_all(asks, "seq", 0, 0, tiled=True)
        slots = jnp.arange(per_owner, dtype=jnp.int32)
        match = (asked[:, 0, None, :] == me) & (asked[:, 2, None, :] == slots[None, :, None])
        picks = jnp.sum(jnp.where(match, asked[:, 1, None, :], 0), axis=-1)
        sent = jnp.take(neighbour_input[0], picks.reshape(-1), axis=0, mode="clip")
        sent = sent.reshape(n_seq, per_owner, NLEN, neighbour_input.shape[-1])
        got = lax.all_to_all(sent, "seq", 0, 0, tiled=True)
        got = got.reshape(n_seq * per_owner, NLEN, neighbour_input.shape[-1])
        chosen_raw = jnp.take(got, owners * per_owner + rank, axis=0, mode="clip")
        chosen = encode_blocks(chosen_raw, enc_gain, full_weights)
        keys_t = jnp.einsum(
            "ef,re->fr", kv_weight[0], chosen, preferred_element_type=jnp.float32
        ).astype(jnp.bfloat16)
        values = jnp.dot(chosen, kv_weight[1], preferred_element_type=jnp.float32).astype(jnp.bfloat16)
        return cross_attend(queries[0], keys_t, values)[None]

    return shards


def solution(mesh):
    return jax.shard_map(
        make_shards(mesh.shape["seq"], mesh.shape["dp"]),
        mesh=mesh,
        in_specs=(
            P("dp", "seq", None),
            P("dp", "seq", None, None),
            P("dp", "seq", None),
            P("dp", "seq", None),
            P(),
            P(None, "dp", None),
            P(),
        ),
        out_specs=P("dp", "seq", None),
        check_vma=False,
    )
```

```python
import jax
import jax.numpy as jnp
from jax import lax
from jax.experimental import pallas as pl
from jax.experimental.pallas import tpu as pltpu
from jax.sharding import PartitionSpec as P

HEADS = 16
HEAD_DIM = 128
ENC_HEADS = 7
NLEN = 64
SPAN = 64
NEIGH = 2
NB_DEV = 4


epsilon = 1e-05


def _softmax_bf16(scores):
    highest = jnp.max(scores, axis=-1, keepdims=True)
    raised = jnp.exp(scores - highest)
    return (raised * (1.0 / jnp.sum(raised, axis=-1, keepdims=True))).astype(jnp.bfloat16)


def _encoder_kernel(x_ref, gain_ref, w_ref, out_ref, q_ref, kt_ref, v_ref, mix_ref):
    inputs = x_ref[...].astype(jnp.float32)
    spread = jnp.mean(inputs * inputs, axis=-1, keepdims=True)
    normed = (inputs * lax.rsqrt(spread + epsilon) * gain_ref[...]).astype(jnp.bfloat16)
    q_ref[...] = jnp.dot(normed, w_ref[0], preferred_element_type=jnp.float32).astype(jnp.bfloat16)
    v_ref[...] = jnp.dot(normed, w_ref[2], preferred_element_type=jnp.float32).astype(jnp.bfloat16)
    kt_ref[...] = jnp.dot(normed, w_ref[1], preferred_element_type=jnp.float32).T.astype(jnp.bfloat16)
    width = inputs.shape[-1]
    head_size = width // ENC_HEADS
    scale = head_size ** (-0.5)
    pair = 2 * NLEN
    rows_of = lax.broadcasted_iota(jnp.int32, (pair, pair), 0) // NLEN
    cols_of = lax.broadcasted_iota(jnp.int32, (pair, pair), 1) // NLEN
    same = rows_of == cols_of
    for b in range(inputs.shape[0] // pair):
        rows = pl.ds(b * pair, pair)
        for h in range(ENC_HEADS):
            cols = pl.ds(h * head_size, head_size)
            scores = jnp.dot(q_ref[rows, cols], kt_ref[cols, rows], preferred_element_type=jnp.float32) * scale
            weights = _softmax_bf16(jnp.where(same, scores, -jnp.inf))
            mix_ref[rows, cols] = jnp.dot(
                weights, v_ref[rows, cols], preferred_element_type=jnp.float32
            ).astype(jnp.bfloat16)
    output = jnp.dot(mix_ref[...], w_ref[3], preferred_element_type=jnp.float32)
    out_ref[...] = (inputs + output).astype(jnp.bfloat16)


def encode_blocks(blocks, gain, attention, group=8):
    count, length, width = blocks.shape
    group = min(group, count)
    rows = group * length
    flat = blocks.reshape(count * length, width)
    return pl.pallas_call(
        _encoder_kernel,
        out_shape=jax.ShapeDtypeStruct(flat.shape, jnp.bfloat16),
        grid=(count // group,),
        in_specs=[
            pl.BlockSpec((rows, width), lambda i: (i, 0)),
            pl.BlockSpec((1, width), lambda i: (0, 0)),
            pl.BlockSpec(attention.shape, lambda i: (0, 0, 0)),
        ],
        out_specs=pl.BlockSpec((rows, width), lambda i: (i, 0)),
        scratch_shapes=[
            pltpu.VMEM((rows, width), jnp.bfloat16),
            pltpu.VMEM((width, rows), jnp.bfloat16),
            pltpu.VMEM((rows, width), jnp.bfloat16),
            pltpu.VMEM((rows, width), jnp.bfloat16),
        ],
    )(flat, gain.reshape(1, width), attention)


def _cross_kernel(q_ref, kt_ref, v_ref, out_ref):
    scale = HEAD_DIM ** (-0.5)
    memory = NEIGH * NLEN
    for s in range(q_ref.shape[0] // SPAN):
        rq = pl.ds(s * SPAN, SPAN)
        rk = pl.ds(s * memory, memory)
        for h in range(q_ref.shape[-1] // HEAD_DIM):
            cols = pl.ds(h * HEAD_DIM, HEAD_DIM)
            scores = jnp.dot(q_ref[rq, cols], kt_ref[cols, rk], preferred_element_type=jnp.float32) * scale
            weights = _softmax_bf16(scores)
            out_ref[rq, cols] = jnp.dot(
                weights, v_ref[rk, cols], preferred_element_type=jnp.float32
            ).astype(jnp.bfloat16)


def cross_attend(queries, keys_t, values, group=4):
    length, width = queries.shape
    memory = NEIGH * NLEN
    group = min(group, length // SPAN)
    return pl.pallas_call(
        _cross_kernel,
        out_shape=jax.ShapeDtypeStruct(queries.shape, jnp.bfloat16),
        grid=(length // (SPAN * group),),
        in_specs=[
            pl.BlockSpec((SPAN * group, width), lambda c: (c, 0)),
            pl.BlockSpec((width, memory * group), lambda c: (0, c)),
            pl.BlockSpec((memory * group, width), lambda c: (c, 0)),
        ],
        out_specs=pl.BlockSpec((SPAN * group, width), lambda c: (c, 0)),
    )(queries, keys_t, values)


def gather_weights(shard, n_dp):
    n_x = n_dp // 2
    place = lax.axis_index("dp")
    x, core = place // 2, place % 2
    pieces = [(shard, place)]
    for shift in range(1, n_x):
        ring = [(src, ((src // 2 + shift) % n_x) * 2 + src % 2) for src in range(n_dp)]
        pieces.append((lax.ppermute(shard, "dp", ring), ((x - shift) % n_x) * 2 + core))
    swap = [(src, src ^ 1) for src in range(n_dp)]
    pieces += [(lax.ppermute(piece, "dp", swap), owner ^ 1) for piece, owner in pieces]
    count, rows, width = shard.shape
    full = jnp.zeros((count, n_dp * rows, width), shard.dtype)
    for piece, owner in pieces:
        full = lax.dynamic_update_slice(full, piece, (0, owner * rows, 0))
    return full


def make_shards(n_seq, n_dp):
    def shards(queries, neighbour_input, owner_list, block_list, enc_gain, enc_attn, kv_weight):
        full_weights = gather_weights(enc_attn, n_dp)
        me = lax.axis_index("seq")
        owners = owner_list.reshape(-1)
        indices = block_list.reshape(-1)
        refs = owners.shape[0]
        per_owner = -(-refs // n_seq)
        same = owners[:, None] == owners[None, :]
        earlier = jnp.arange(refs)[None, :] < jnp.arange(refs)[:, None]
        rank = jnp.sum(same & earlier, axis=1).astype(jnp.int32)
        asks = jnp.stack([owners, indices, rank])
        asks = jnp.broadcast_to(asks[None], (n_seq, 3, refs))
        asked = lax.all_to_all(asks, "seq", 0, 0, tiled=True)
        slots = jnp.arange(per_owner, dtype=jnp.int32)
        match = (asked[:, 0, None, :] == me) & (asked[:, 2, None, :] == slots[None, :, None])
        picks = jnp.sum(jnp.where(match, asked[:, 1, None, :], 0), axis=-1)
        own = neighbour_input[0]
        sent = jnp.zeros((n_seq, per_owner) + own.shape[1:], own.dtype)
        for block in range(own.shape[0]):
            sent = jnp.where((picks == block)[:, :, None, None], own[block], sent)
        got = lax.all_to_all(sent, "seq", 0, 0, tiled=True)
        got = got.reshape(n_seq * per_owner, NLEN, neighbour_input.shape[-1])
        chosen_raw = jnp.take(got, owners * per_owner + rank, axis=0, mode="clip")
        chosen = encode_blocks(chosen_raw, enc_gain, full_weights)
        keys_t = jnp.einsum(
            "ef,re->fr", kv_weight[0], chosen, preferred_element_type=jnp.float32
        ).astype(jnp.bfloat16)
        values = jnp.dot(chosen, kv_weight[1], preferred_element_type=jnp.float32).astype(jnp.bfloat16)
        return cross_attend(queries[0], keys_t, values)[None]

    return shards


def solution(mesh):
    return jax.shard_map(
        make_shards(mesh.shape["seq"], mesh.shape["dp"]),
        mesh=mesh,
        in_specs=(
            P("dp", "seq", None),
            P("dp", "seq", None, None),
            P("dp", "seq", None),
            P("dp", "seq", None),
            P(),
            P(None, "dp", None),
            P(),
        ),
        out_specs=P("dp", "seq", None),
        check_vma=False,
    )
```

```python
import jax
import jax.numpy as jnp
from jax import lax
from jax.experimental import pallas as pl
from jax.experimental.pallas import tpu as pltpu
from jax.sharding import PartitionSpec as P

HEADS = 16
HEAD_DIM = 128
ENC_HEADS = 7
NLEN = 64
SPAN = 64
NEIGH = 2
NB_DEV = 4


epsilon = 1e-05


def _softmax_bf16(scores):
    highest = jnp.max(scores, axis=-1, keepdims=True)
    raised = jnp.exp(scores - highest)
    return (raised * (1.0 / jnp.sum(raised, axis=-1, keepdims=True))).astype(jnp.bfloat16)


def _encoder_kernel(x_ref, gain_ref, w_ref, out_ref, q_ref, kt_ref, v_ref, mix_ref):
    inputs = x_ref[...].astype(jnp.float32)
    spread = jnp.mean(inputs * inputs, axis=-1, keepdims=True)
    normed = (inputs * lax.rsqrt(spread + epsilon) * gain_ref[...]).astype(jnp.bfloat16)
    q_ref[...] = jnp.dot(normed, w_ref[0], preferred_element_type=jnp.float32).astype(jnp.bfloat16)
    v_ref[...] = jnp.dot(normed, w_ref[2], preferred_element_type=jnp.float32).astype(jnp.bfloat16)
    kt_ref[...] = jnp.dot(normed, w_ref[1], preferred_element_type=jnp.float32).T.astype(jnp.bfloat16)
    width = inputs.shape[-1]
    head_size = width // ENC_HEADS
    scale = head_size ** (-0.5)
    pair = 2 * NLEN
    rows_of = lax.broadcasted_iota(jnp.int32, (pair, pair), 0) // NLEN
    cols_of = lax.broadcasted_iota(jnp.int32, (pair, pair), 1) // NLEN
    same = rows_of == cols_of
    for b in range(inputs.shape[0] // pair):
        rows = pl.ds(b * pair, pair)
        for h in range(ENC_HEADS):
            cols = pl.ds(h * head_size, head_size)
            scores = jnp.dot(q_ref[rows, cols], kt_ref[cols, rows], preferred_element_type=jnp.float32) * scale
            weights = _softmax_bf16(jnp.where(same, scores, -jnp.inf))
            mix_ref[rows, cols] = jnp.dot(
                weights, v_ref[rows, cols], preferred_element_type=jnp.float32
            ).astype(jnp.bfloat16)
    output = jnp.dot(mix_ref[...], w_ref[3], preferred_element_type=jnp.float32)
    out_ref[...] = (inputs + output).astype(jnp.bfloat16)


def encode_blocks(blocks, gain, attention, group=8):
    count, length, width = blocks.shape
    group = min(group, count)
    rows = group * length
    flat = blocks.reshape(count * length, width)
    return pl.pallas_call(
        _encoder_kernel,
        out_shape=jax.ShapeDtypeStruct(flat.shape, jnp.bfloat16),
        grid=(count // group,),
        in_specs=[
            pl.BlockSpec((rows, width), lambda i: (i, 0)),
            pl.BlockSpec((1, width), lambda i: (0, 0)),
            pl.BlockSpec(attention.shape, lambda i: (0, 0, 0)),
        ],
        out_specs=pl.BlockSpec((rows, width), lambda i: (i, 0)),
        scratch_shapes=[
            pltpu.VMEM((rows, width), jnp.bfloat16),
            pltpu.VMEM((width, rows), jnp.bfloat16),
            pltpu.VMEM((rows, width), jnp.bfloat16),
            pltpu.VMEM((rows, width), jnp.bfloat16),
        ],
    )(flat, gain.reshape(1, width), attention)


def _cross_kernel(qt_ref, k_ref, v_ref, out_ref):
    scale = HEAD_DIM ** (-0.5)
    spans, memory = 2 * SPAN, 2 * NEIGH * NLEN
    key_of = lax.broadcasted_iota(jnp.int32, (memory, spans), 0) // (NEIGH * NLEN)
    query_of = lax.broadcasted_iota(jnp.int32, (memory, spans), 1) // SPAN
    same = key_of == query_of
    for p in range(qt_ref.shape[-1] // spans):
        rq = pl.ds(p * spans, spans)
        rk = pl.ds(p * memory, memory)
        for h in range(k_ref.shape[-1] // HEAD_DIM):
            cols = pl.ds(h * HEAD_DIM, HEAD_DIM)
            scores = jnp.dot(k_ref[rk, cols], qt_ref[cols, rq], preferred_element_type=jnp.float32) * scale
            scores = jnp.where(same, scores, -jnp.inf)
            highest = jnp.max(scores, axis=0, keepdims=True)
            raised = jnp.exp(scores - highest)
            weights = (raised * (1.0 / jnp.sum(raised, axis=0, keepdims=True))).astype(jnp.bfloat16)
            out_ref[rq, cols] = lax.dot_general(
                weights, v_ref[rk, cols], (((0,), (0,)), ((), ())), preferred_element_type=jnp.float32
            ).astype(jnp.bfloat16)


def cross_attend(queries_t, keys, values, group=2):
    width, length = queries_t.shape
    spans = 2 * SPAN
    memory = 2 * NEIGH * NLEN
    group = min(group, length // spans)
    return pl.pallas_call(
        _cross_kernel,
        out_shape=jax.ShapeDtypeStruct((length, width), jnp.bfloat16),
        grid=(length // (spans * group),),
        in_specs=[
            pl.BlockSpec((width, spans * group), lambda c: (0, c)),
            pl.BlockSpec((memory * group, width), lambda c: (c, 0)),
            pl.BlockSpec((memory * group, width), lambda c: (c, 0)),
        ],
        out_specs=pl.BlockSpec((spans * group, width), lambda c: (c, 0)),
    )(queries_t, keys, values)


def gather_weights(shard, n_dp):
    n_x = n_dp // 2
    place = lax.axis_index("dp")
    x, core = place // 2, place % 2
    pieces = [(shard, place)]
    for shift in range(1, n_x):
        ring = [(src, ((src // 2 + shift) % n_x) * 2 + src % 2) for src in range(n_dp)]
        pieces.append((lax.ppermute(shard, "dp", ring), ((x - shift) % n_x) * 2 + core))
    swap = [(src, src ^ 1) for src in range(n_dp)]
    pieces += [(lax.ppermute(piece, "dp", swap), owner ^ 1) for piece, owner in pieces]
    count, rows, width = shard.shape
    full = jnp.zeros((count, n_dp * rows, width), shard.dtype)
    for piece, owner in pieces:
        full = lax.dynamic_update_slice(full, piece, (0, owner * rows, 0))
    return full


def make_shards(n_seq, n_dp):
    def shards(queries, neighbour_input, owner_list, block_list, enc_gain, enc_attn, kv_weight):
        full_weights = gather_weights(enc_attn, n_dp)
        me = lax.axis_index("seq")
        owners = owner_list.reshape(-1)
        indices = block_list.reshape(-1)
        refs = owners.shape[0]
        per_owner = -(-refs // n_seq)
        same = owners[:, None] == owners[None, :]
        earlier = jnp.arange(refs)[None, :] < jnp.arange(refs)[:, None]
        rank = jnp.sum(same & earlier, axis=1).astype(jnp.int32)
        asks = jnp.stack([owners, indices, rank])
        asks = jnp.broadcast_to(asks[None], (n_seq, 3, refs))
        asked = lax.all_to_all(asks, "seq", 0, 0, tiled=True)
        slots = jnp.arange(per_owner, dtype=jnp.int32)
        match = (asked[:, 0, None, :] == me) & (asked[:, 2, None, :] == slots[None, :, None])
        picks = jnp.sum(jnp.where(match, asked[:, 1, None, :], 0), axis=-1)
        sent = jnp.take(neighbour_input[0], picks.reshape(-1), axis=0, mode="clip")
        sent = sent.reshape(n_seq, per_owner, NLEN, neighbour_input.shape[-1])
        got = lax.all_to_all(sent, "seq", 0, 0, tiled=True)
        got = got.reshape(n_seq * per_owner, NLEN, neighbour_input.shape[-1])
        chosen_raw = jnp.take(got, owners * per_owner + rank, axis=0, mode="clip")
        chosen = encode_blocks(chosen_raw, enc_gain, full_weights)
        keys = jnp.dot(chosen, kv_weight[0], preferred_element_type=jnp.float32).astype(jnp.bfloat16)
        values = jnp.dot(chosen, kv_weight[1], preferred_element_type=jnp.float32).astype(jnp.bfloat16)
        return cross_attend(queries[0].T, keys, values)[None]

    return shards


def solution(mesh):
    return jax.shard_map(
        make_shards(mesh.shape["seq"], mesh.shape["dp"]),
        mesh=mesh,
        in_specs=(
            P("dp", "seq", None),
            P("dp", "seq", None, None),
            P("dp", "seq", None),
            P("dp", "seq", None),
            P(),
            P(None, "dp", None),
            P(),
        ),
        out_specs=P("dp", "seq", None),
        check_vma=False,
    )
```

```python
import jax
import jax.numpy as jnp
from jax import lax
from jax.experimental import pallas as pl
from jax.experimental.pallas import tpu as pltpu
from jax.sharding import PartitionSpec as P

HEADS = 16
HEAD_DIM = 128
ENC_HEADS = 7
NLEN = 64
SPAN = 64
NEIGH = 2
NB_DEV = 4


epsilon = 1e-05


def _softmax_bf16(scores):
    highest = jnp.max(scores, axis=-1, keepdims=True)
    raised = jnp.exp(scores - highest)
    return (raised * (1.0 / jnp.sum(raised, axis=-1, keepdims=True))).astype(jnp.bfloat16)


def _encoder_kernel(x_ref, gain_ref, w_ref, out_ref, q_ref, kt_ref, v_ref, mix_ref):
    inputs = x_ref[...].astype(jnp.float32)
    spread = jnp.mean(inputs * inputs, axis=-1, keepdims=True)
    normed = (inputs * lax.rsqrt(spread + epsilon) * gain_ref[...]).astype(jnp.bfloat16)
    q_ref[...] = jnp.dot(normed, w_ref[0], preferred_element_type=jnp.float32).astype(jnp.bfloat16)
    v_ref[...] = jnp.dot(normed, w_ref[2], preferred_element_type=jnp.float32).astype(jnp.bfloat16)
    kt_ref[...] = jnp.dot(normed, w_ref[1], preferred_element_type=jnp.float32).T.astype(jnp.bfloat16)
    width = inputs.shape[-1]
    head_size = width // ENC_HEADS
    scale = head_size ** (-0.5)
    pair = 2 * NLEN
    rows_of = lax.broadcasted_iota(jnp.int32, (pair, pair), 0) // NLEN
    cols_of = lax.broadcasted_iota(jnp.int32, (pair, pair), 1) // NLEN
    same = rows_of == cols_of
    for b in range(inputs.shape[0] // pair):
        rows = pl.ds(b * pair, pair)
        for h in range(ENC_HEADS):
            cols = pl.ds(h * head_size, head_size)
            scores = jnp.dot(q_ref[rows, cols], kt_ref[cols, rows], preferred_element_type=jnp.float32) * scale
            weights = _softmax_bf16(jnp.where(same, scores, -jnp.inf))
            mix_ref[rows, cols] = jnp.dot(
                weights, v_ref[rows, cols], preferred_element_type=jnp.float32
            ).astype(jnp.bfloat16)
    output = jnp.dot(mix_ref[...], w_ref[3], preferred_element_type=jnp.float32)
    out_ref[...] = (inputs + output).astype(jnp.bfloat16)


def encode_blocks(blocks, gain, attention, group=8):
    count, length, width = blocks.shape
    group = min(group, count)
    rows = group * length
    flat = blocks.reshape(count * length, width)
    return pl.pallas_call(
        _encoder_kernel,
        out_shape=jax.ShapeDtypeStruct(flat.shape, jnp.bfloat16),
        grid=(count // group,),
        in_specs=[
            pl.BlockSpec((rows, width), lambda i: (i, 0)),
            pl.BlockSpec((1, width), lambda i: (0, 0)),
            pl.BlockSpec(attention.shape, lambda i: (0, 0, 0)),
        ],
        out_specs=pl.BlockSpec((rows, width), lambda i: (i, 0)),
        scratch_shapes=[
            pltpu.VMEM((rows, width), jnp.bfloat16),
            pltpu.VMEM((width, rows), jnp.bfloat16),
            pltpu.VMEM((rows, width), jnp.bfloat16),
            pltpu.VMEM((rows, width), jnp.bfloat16),
        ],
    )(flat, gain.reshape(1, width), attention)


def _cross_kernel(q_ref, kt_ref, v_ref, out_ref):
    scale = HEAD_DIM ** (-0.5)
    memory = NEIGH * NLEN
    for s in range(q_ref.shape[0] // SPAN):
        rq = pl.ds(s * SPAN, SPAN)
        rk = pl.ds(s * memory, memory)
        for h in range(q_ref.shape[-1] // HEAD_DIM):
            cols = pl.ds(h * HEAD_DIM, HEAD_DIM)
            scores = jnp.dot(q_ref[rq, cols], kt_ref[cols, rk], preferred_element_type=jnp.float32) * scale
            weights = _softmax_bf16(scores)
            out_ref[rq, cols] = jnp.dot(
                weights, v_ref[rk, cols], preferred_element_type=jnp.float32
            ).astype(jnp.bfloat16)


def cross_attend(queries, keys_t, values, group=4):
    length, width = queries.shape
    memory = NEIGH * NLEN
    group = min(group, length // SPAN)
    return pl.pallas_call(
        _cross_kernel,
        out_shape=jax.ShapeDtypeStruct(queries.shape, jnp.bfloat16),
        grid=(length // (SPAN * group),),
        in_specs=[
            pl.BlockSpec((SPAN * group, width), lambda c: (c, 0)),
            pl.BlockSpec((width, memory * group), lambda c: (0, c)),
            pl.BlockSpec((memory * group, width), lambda c: (c, 0)),
        ],
        out_specs=pl.BlockSpec((SPAN * group, width), lambda c: (c, 0)),
    )(queries, keys_t, values)


def gather_weights(shard, n_dp):
    n_x = n_dp // 2
    place = lax.axis_index("dp")
    x, core = place // 2, place % 2
    pieces = [(shard, place)]
    for shift in range(1, n_x):
        ring = [(src, ((src // 2 + shift) % n_x) * 2 + src % 2) for src in range(n_dp)]
        pieces.append((lax.ppermute(shard, "dp", ring), ((x - shift) % n_x) * 2 + core))
    swap = [(src, src ^ 1) for src in range(n_dp)]
    pieces += [(lax.ppermute(piece, "dp", swap), owner ^ 1) for piece, owner in pieces]
    count, rows, width = shard.shape
    full = jnp.zeros((count, n_dp * rows, width), shard.dtype)
    for piece, owner in pieces:
        full = lax.dynamic_update_slice(full, piece, (0, owner * rows, 0))
    return full


def make_shards(n_seq, n_dp):
    def shards(queries, neighbour_input, owner_list, block_list, enc_gain, enc_attn, kv_weight):
        full_weights = gather_weights(enc_attn, n_dp)
        me = lax.axis_index("seq")
        owners = owner_list.reshape(-1)
        indices = block_list.reshape(-1)
        refs = owners.shape[0]
        per_owner = -(-refs // n_seq)
        earlier = jnp.arange(refs)[None, :] < jnp.arange(refs)[:, None]

        def rank_of(names):
            return jnp.sum((names[..., :, None] == names[..., None, :]) & earlier, axis=-1)

        asks = jnp.concatenate([owner_list, block_list], axis=0)
        asks = jnp.broadcast_to(asks[None], (n_seq,) + asks.shape)
        asked = lax.all_to_all(asks, "seq", 0, 0, tiled=True).reshape(n_seq, 2, refs)
        rank = rank_of(owners).astype(jnp.int32)
        asked_rank = rank_of(asked[:, 0])
        slots = jnp.arange(per_owner, dtype=jnp.int32)
        match = (asked[:, 0, None, :] == me) & (asked_rank[:, None, :] == slots[None, :, None])
        picks = jnp.sum(jnp.where(match, asked[:, 1, None, :], 0), axis=-1)
        sent = jnp.take(neighbour_input[0], picks.reshape(-1), axis=0, mode="clip")
        sent = sent.reshape(n_seq, per_owner, NLEN, neighbour_input.shape[-1])
        got = lax.all_to_all(sent, "seq", 0, 0, tiled=True)
        got = got.reshape(n_seq * per_owner, NLEN, neighbour_input.shape[-1])
        chosen_raw = jnp.take(got, owners * per_owner + rank, axis=0, mode="clip")
        chosen = encode_blocks(chosen_raw, enc_gain, full_weights)
        keys_t = jnp.einsum(
            "ef,re->fr", kv_weight[0], chosen, preferred_element_type=jnp.float32
        ).astype(jnp.bfloat16)
        values = jnp.dot(chosen, kv_weight[1], preferred_element_type=jnp.float32).astype(jnp.bfloat16)
        return cross_attend(queries[0], keys_t, values)[None]

    return shards


def solution(mesh):
    return jax.shard_map(
        make_shards(mesh.shape["seq"], mesh.shape["dp"]),
        mesh=mesh,
        in_specs=(
            P("dp", "seq", None),
            P("dp", "seq", None, None),
            P("dp", "seq", None),
            P("dp", "seq", None),
            P(),
            P(None, "dp", None),
            P(),
        ),
        out_specs=P("dp", "seq", None),
        check_vma=False,
    )
```

```python
import jax
import jax.numpy as jnp
from jax import lax
from jax.experimental import pallas as pl
from jax.experimental.pallas import tpu as pltpu
from jax.sharding import PartitionSpec as P

HEADS = 16
HEAD_DIM = 128
ENC_HEADS = 7
NLEN = 64
SPAN = 64
NEIGH = 2
NB_DEV = 4


epsilon = 1e-05


def _softmax_bf16(scores):
    highest = jnp.max(scores, axis=-1, keepdims=True)
    raised = jnp.exp(scores - highest)
    return (raised * (1.0 / jnp.sum(raised, axis=-1, keepdims=True))).astype(jnp.bfloat16)


def _encoder_kernel(x_ref, gain_ref, w_ref, out_ref, q_ref, kt_ref, v_ref, mix_ref):
    inputs = x_ref[...].astype(jnp.float32)
    spread = jnp.mean(inputs * inputs, axis=-1, keepdims=True)
    normed = (inputs * lax.rsqrt(spread + epsilon) * gain_ref[...]).astype(jnp.bfloat16)
    q_ref[...] = jnp.dot(normed, w_ref[0], preferred_element_type=jnp.float32).astype(jnp.bfloat16)
    v_ref[...] = jnp.dot(normed, w_ref[2], preferred_element_type=jnp.float32).astype(jnp.bfloat16)
    kt_ref[...] = jnp.dot(normed, w_ref[1], preferred_element_type=jnp.float32).astype(jnp.bfloat16).T
    width = inputs.shape[-1]
    head_size = width // ENC_HEADS
    scale = head_size ** (-0.5)
    pair = 2 * NLEN
    rows_of = lax.broadcasted_iota(jnp.int32, (pair, pair), 0) // NLEN
    cols_of = lax.broadcasted_iota(jnp.int32, (pair, pair), 1) // NLEN
    same = rows_of == cols_of
    for b in range(inputs.shape[0] // pair):
        rows = pl.ds(b * pair, pair)
        for h in range(ENC_HEADS):
            cols = pl.ds(h * head_size, head_size)
            scores = jnp.dot(q_ref[rows, cols], kt_ref[cols, rows], preferred_element_type=jnp.float32) * scale
            weights = _softmax_bf16(jnp.where(same, scores, -jnp.inf))
            mix_ref[rows, cols] = jnp.dot(
                weights, v_ref[rows, cols], preferred_element_type=jnp.float32
            ).astype(jnp.bfloat16)
    output = jnp.dot(mix_ref[...], w_ref[3], preferred_element_type=jnp.float32)
    out_ref[...] = (inputs + output).astype(jnp.bfloat16)


def encode_blocks(blocks, gain, attention, group=8):
    count, length, width = blocks.shape
    group = min(group, count)
    rows = group * length
    flat = blocks.reshape(count * length, width)
    return pl.pallas_call(
        _encoder_kernel,
        out_shape=jax.ShapeDtypeStruct(flat.shape, jnp.bfloat16),
        grid=(count // group,),
        in_specs=[
            pl.BlockSpec((rows, width), lambda i: (i, 0)),
            pl.BlockSpec((1, width), lambda i: (0, 0)),
            pl.BlockSpec(attention.shape, lambda i: (0, 0, 0)),
        ],
        out_specs=pl.BlockSpec((rows, width), lambda i: (i, 0)),
        scratch_shapes=[
            pltpu.VMEM((rows, width), jnp.bfloat16),
            pltpu.VMEM((width, rows), jnp.bfloat16),
            pltpu.VMEM((rows, width), jnp.bfloat16),
            pltpu.VMEM((rows, width), jnp.bfloat16),
        ],
    )(flat, gain.reshape(1, width), attention)


def _cross_kernel(q_ref, kt_ref, v_ref, out_ref):
    scale = HEAD_DIM ** (-0.5)
    memory = NEIGH * NLEN
    for s in range(q_ref.shape[0] // SPAN):
        rq = pl.ds(s * SPAN, SPAN)
        rk = pl.ds(s * memory, memory)
        for h in range(q_ref.shape[-1] // HEAD_DIM):
            cols = pl.ds(h * HEAD_DIM, HEAD_DIM)
            scores = jnp.dot(q_ref[rq, cols], kt_ref[cols, rk], preferred_element_type=jnp.float32) * scale
            weights = _softmax_bf16(scores)
            out_ref[rq, cols] = jnp.dot(
                weights, v_ref[rk, cols], preferred_element_type=jnp.float32
            ).astype(jnp.bfloat16)


def cross_attend(queries, keys_t, values, group=4):
    length, width = queries.shape
    memory = NEIGH * NLEN
    group = min(group, length // SPAN)
    return pl.pallas_call(
        _cross_kernel,
        out_shape=jax.ShapeDtypeStruct(queries.shape, jnp.bfloat16),
        grid=(length // (SPAN * group),),
        in_specs=[
            pl.BlockSpec((SPAN * group, width), lambda c: (c, 0)),
            pl.BlockSpec((width, memory * group), lambda c: (0, c)),
            pl.BlockSpec((memory * group, width), lambda c: (c, 0)),
        ],
        out_specs=pl.BlockSpec((SPAN * group, width), lambda c: (c, 0)),
    )(queries, keys_t, values)


def gather_weights(shard, n_dp):
    n_x = n_dp // 2
    place = lax.axis_index("dp")
    x, core = place // 2, place % 2
    pieces = [(shard, place)]
    for shift in range(1, n_x):
        ring = [(src, ((src // 2 + shift) % n_x) * 2 + src % 2) for src in range(n_dp)]
        pieces.append((lax.ppermute(shard, "dp", ring), ((x - shift) % n_x) * 2 + core))
    swap = [(src, src ^ 1) for src in range(n_dp)]
    pieces += [(lax.ppermute(piece, "dp", swap), owner ^ 1) for piece, owner in pieces]
    count, rows, width = shard.shape
    full = jnp.zeros((count, n_dp * rows, width), shard.dtype)
    for piece, owner in pieces:
        full = lax.dynamic_update_slice(full, piece, (0, owner * rows, 0))
    return full


def make_shards(n_seq, n_dp):
    def shards(queries, neighbour_input, owner_list, block_list, enc_gain, enc_attn, kv_weight):
        full_weights = gather_weights(enc_attn, n_dp)
        me = lax.axis_index("seq")
        owners = owner_list.reshape(-1)
        indices = block_list.reshape(-1)
        refs = owners.shape[0]
        per_owner = -(-refs // n_seq)
        same = owners[:, None] == owners[None, :]
        earlier = jnp.arange(refs)[None, :] < jnp.arange(refs)[:, None]
        rank = jnp.sum(same & earlier, axis=1).astype(jnp.int32)
        asks = jnp.stack([owners, indices, rank])
        asks = jnp.broadcast_to(asks[None], (n_seq, 3, refs))
        asked = lax.all_to_all(asks, "seq", 0, 0, tiled=True)
        slots = jnp.arange(per_owner, dtype=jnp.int32)
        match = (asked[:, 0, None, :] == me) & (asked[:, 2, None, :] == slots[None, :, None])
        picks = jnp.sum(jnp.where(match, asked[:, 1, None, :], 0), axis=-1)
        sent = jnp.take(neighbour_input[0], picks.reshape(-1), axis=0, mode="clip")
        sent = sent.reshape(n_seq, per_owner, NLEN, neighbour_input.shape[-1])
        got = lax.all_to_all(sent, "seq", 0, 0, tiled=True)
        got = got.reshape(n_seq * per_owner, NLEN, neighbour_input.shape[-1])
        chosen_raw = jnp.take(got, owners * per_owner + rank, axis=0, mode="clip")
        chosen = encode_blocks(chosen_raw, enc_gain, full_weights)
        keys_t = jnp.einsum(
            "ef,re->fr", kv_weight[0], chosen, preferred_element_type=jnp.float32
        ).astype(jnp.bfloat16)
        values = jnp.dot(chosen, kv_weight[1], preferred_element_type=jnp.float32).astype(jnp.bfloat16)
        return cross_attend(queries[0], keys_t, values)[None]

    return shards


def solution(mesh):
    return jax.shard_map(
        make_shards(mesh.shape["seq"], mesh.shape["dp"]),
        mesh=mesh,
        in_specs=(
            P("dp", "seq", None),
            P("dp", "seq", None, None),
            P("dp", "seq", None),
            P("dp", "seq", None),
            P(),
            P(None, "dp", None),
            P(),
        ),
        out_specs=P("dp", "seq", None),
        check_vma=False,
    )
```

```python
import jax
import jax.numpy as jnp
from jax import lax
from jax.experimental import pallas as pl
from jax.experimental.pallas import tpu as pltpu
from jax.sharding import PartitionSpec as P

HEADS = 16
HEAD_DIM = 128
ENC_HEADS = 7
NLEN = 64
SPAN = 64
NEIGH = 2
NB_DEV = 4


epsilon = 1e-05


def _softmax_bf16(scores):
    highest = jnp.max(scores, axis=-1, keepdims=True)
    raised = jnp.exp(scores - highest)
    return (raised * (1.0 / jnp.sum(raised, axis=-1, keepdims=True))).astype(jnp.bfloat16)


def _encoder_kernel(x_ref, gain_ref, w_ref, out_ref, q_ref, kt_ref, v_ref, mix_ref):
    inputs = x_ref[...].astype(jnp.float32)
    spread = jnp.mean(inputs * inputs, axis=-1, keepdims=True)
    normed = (inputs * lax.rsqrt(spread + epsilon) * gain_ref[...]).astype(jnp.bfloat16)
    q_ref[...] = jnp.dot(normed, w_ref[0], preferred_element_type=jnp.float32).astype(jnp.bfloat16)
    v_ref[...] = jnp.dot(normed, w_ref[2], preferred_element_type=jnp.float32).astype(jnp.bfloat16)
    kt_ref[...] = jnp.dot(normed, w_ref[1], preferred_element_type=jnp.float32).astype(jnp.bfloat16).T
    width = inputs.shape[-1]
    head_size = width // ENC_HEADS
    scale = head_size ** (-0.5)
    pair = 2 * NLEN
    rows_of = lax.broadcasted_iota(jnp.int32, (pair, pair), 0) // NLEN
    cols_of = lax.broadcasted_iota(jnp.int32, (pair, pair), 1) // NLEN
    same = rows_of == cols_of
    for b in range(inputs.shape[0] // pair):
        rows = pl.ds(b * pair, pair)
        for h in range(ENC_HEADS):
            cols = pl.ds(h * head_size, head_size)
            scores = jnp.dot(q_ref[rows, cols], kt_ref[cols, rows], preferred_element_type=jnp.float32) * scale
            weights = _softmax_bf16(jnp.where(same, scores, -jnp.inf))
            mix_ref[rows, cols] = jnp.dot(
                weights, v_ref[rows, cols], preferred_element_type=jnp.float32
            ).astype(jnp.bfloat16)
    output = jnp.dot(mix_ref[...], w_ref[3], preferred_element_type=jnp.float32)
    out_ref[...] = (inputs + output).astype(jnp.bfloat16)


def encode_blocks(blocks, gain, attention, group=8):
    count, length, width = blocks.shape
    group = min(group, count)
    rows = group * length
    flat = blocks.reshape(count * length, width)
    return pl.pallas_call(
        _encoder_kernel,
        out_shape=jax.ShapeDtypeStruct(flat.shape, jnp.bfloat16),
        grid=(count // group,),
        in_specs=[
            pl.BlockSpec((rows, width), lambda i: (i, 0)),
            pl.BlockSpec((1, width), lambda i: (0, 0)),
            pl.BlockSpec(attention.shape, lambda i: (0, 0, 0)),
        ],
        out_specs=pl.BlockSpec((rows, width), lambda i: (i, 0)),
        scratch_shapes=[
            pltpu.VMEM((rows, width), jnp.bfloat16),
            pltpu.VMEM((width, rows), jnp.bfloat16),
            pltpu.VMEM((rows, width), jnp.bfloat16),
            pltpu.VMEM((rows, width), jnp.bfloat16),
        ],
    )(flat, gain.reshape(1, width), attention)


def _cross_kernel(slot_ref, qt_ref, *refs):
    count = (len(refs) - 1) // 2
    k_refs, v_refs, out_ref = refs[:count], refs[count:2 * count], refs[-1]
    scale = HEAD_DIM ** (-0.5)
    spans, memory = 2 * SPAN, 2 * NEIGH * NLEN
    key_of = lax.broadcasted_iota(jnp.int32, (memory, spans), 0) // (NEIGH * NLEN)
    query_of = lax.broadcasted_iota(jnp.int32, (memory, spans), 1) // SPAN
    same = key_of == query_of
    for h in range(qt_ref.shape[0] // HEAD_DIM):
        cols = pl.ds(h * HEAD_DIM, HEAD_DIM)
        queries_t = qt_ref[cols, :]
        scores = jnp.concatenate(
            [jnp.dot(k[0, :, cols], queries_t, preferred_element_type=jnp.float32) for k in k_refs], axis=0
        ) * scale
        scores = jnp.where(same, scores, -jnp.inf)
        highest = jnp.max(scores, axis=0, keepdims=True)
        raised = jnp.exp(scores - highest)
        weights = (raised * (1.0 / jnp.sum(raised, axis=0, keepdims=True))).astype(jnp.bfloat16)
        mixed = lax.dot_general(
            weights[:NLEN], v_refs[0][0, :, cols], (((0,), (0,)), ((), ())), preferred_element_type=jnp.float32
        )
        for j in range(1, count):
            mixed = mixed + lax.dot_general(
                weights[j * NLEN:(j + 1) * NLEN], v_refs[j][0, :, cols],
                (((0,), (0,)), ((), ())), preferred_element_type=jnp.float32,
            )
        out_ref[:, cols] = mixed.astype(jnp.bfloat16)


def cross_attend(queries_t, keys, values, slots):
    width, length = queries_t.shape
    spans = 2 * SPAN
    count = 2 * NEIGH
    slots = jnp.clip(slots, 0, keys.shape[0] - 1).astype(jnp.int32)

    def block_spec(j):
        return pl.BlockSpec((1, NLEN, width), lambda c, slot_ref: (slot_ref[c * count + j], 0, 0))

    grid_spec = pltpu.PrefetchScalarGridSpec(
        num_scalar_prefetch=1,
        grid=(length // spans,),
        in_specs=[pl.BlockSpec((width, spans), lambda c, slot_ref: (0, c))]
        + [block_spec(j) for j in range(count)]
        + [block_spec(j) for j in range(count)],
        out_specs=pl.BlockSpec((spans, width), lambda c, slot_ref: (c, 0)),
    )
    return pl.pallas_call(
        _cross_kernel,
        out_shape=jax.ShapeDtypeStruct((length, width), jnp.bfloat16),
        grid_spec=grid_spec,
    )(slots, queries_t, *([keys] * count), *([values] * count))


def gather_weights(shard, n_dp):
    n_x = n_dp // 2
    place = lax.axis_index("dp")
    x, core = place // 2, place % 2
    pieces = [(shard, place)]
    for shift in range(1, n_x):
        ring = [(src, ((src // 2 + shift) % n_x) * 2 + src % 2) for src in range(n_dp)]
        pieces.append((lax.ppermute(shard, "dp", ring), ((x - shift) % n_x) * 2 + core))
    swap = [(src, src ^ 1) for src in range(n_dp)]
    pieces += [(lax.ppermute(piece, "dp", swap), owner ^ 1) for piece, owner in pieces]
    count, rows, width = shard.shape
    full = jnp.zeros((count, n_dp * rows, width), shard.dtype)
    for piece, owner in pieces:
        full = lax.dynamic_update_slice(full, piece, (0, owner * rows, 0))
    return full


def make_shards(n_seq, n_dp):
    def shards(queries, neighbour_input, owner_list, block_list, enc_gain, enc_attn, kv_weight):
        full_weights = gather_weights(enc_attn, n_dp)
        me = lax.axis_index("seq")
        owners = owner_list.reshape(-1)
        indices = block_list.reshape(-1)
        refs = owners.shape[0]
        per_owner = -(-refs // n_seq)
        same = owners[:, None] == owners[None, :]
        earlier = jnp.arange(refs)[None, :] < jnp.arange(refs)[:, None]
        rank = jnp.sum(same & earlier, axis=1).astype(jnp.int32)
        asks = jnp.stack([owners, indices, rank])
        asks = jnp.broadcast_to(asks[None], (n_seq, 3, refs))
        asked = lax.all_to_all(asks, "seq", 0, 0, tiled=True)
        slots = jnp.arange(per_owner, dtype=jnp.int32)
        match = (asked[:, 0, None, :] == me) & (asked[:, 2, None, :] == slots[None, :, None])
        picks = jnp.sum(jnp.where(match, asked[:, 1, None, :], 0), axis=-1)
        sent = jnp.take(neighbour_input[0], picks.reshape(-1), axis=0, mode="clip")
        sent = sent.reshape(n_seq, per_owner, NLEN, neighbour_input.shape[-1])
        got = lax.all_to_all(sent, "seq", 0, 0, tiled=True)
        got = got.reshape(n_seq * per_owner, NLEN, neighbour_input.shape[-1])
        slots = owners * per_owner + rank
        if got.shape[0] > refs:
            got = jnp.take(got, slots, axis=0, mode="clip")
            slots = jnp.arange(refs, dtype=jnp.int32)
        chosen = encode_blocks(got, enc_gain, full_weights)
        keys = jnp.dot(chosen, kv_weight[0], preferred_element_type=jnp.float32).astype(jnp.bfloat16)
        values = jnp.dot(chosen, kv_weight[1], preferred_element_type=jnp.float32).astype(jnp.bfloat16)
        blocks = (got.shape[0], NLEN, keys.shape[-1])
        return cross_attend(queries[0].T, keys.reshape(blocks), values.reshape(blocks), slots)[None]

    return shards


def solution(mesh):
    return jax.shard_map(
        make_shards(mesh.shape["seq"], mesh.shape["dp"]),
        mesh=mesh,
        in_specs=(
            P("dp", "seq", None),
            P("dp", "seq", None, None),
            P("dp", "seq", None),
            P("dp", "seq", None),
            P(),
            P(None, "dp", None),
            P(),
        ),
        out_specs=P("dp", "seq", None),
        check_vma=False,
    )
```

```python
import jax
import jax.numpy as jnp
from jax import lax
from jax.experimental import pallas as pl
from jax.experimental.pallas import tpu as pltpu
from jax.sharding import PartitionSpec as P

HEADS = 16
HEAD_DIM = 128
ENC_HEADS = 7
NLEN = 64
SPAN = 64
NEIGH = 2
NB_DEV = 4


epsilon = 1e-05


def _softmax_bf16(scores):
    highest = jnp.max(scores, axis=-1, keepdims=True)
    raised = jnp.exp(scores - highest)
    return (raised * (1.0 / jnp.sum(raised, axis=-1, keepdims=True))).astype(jnp.bfloat16)


def _encoder_kernel(x_ref, gain_ref, w_ref, out_ref, q_ref, kt_ref, v_ref, mix_ref):
    inputs = x_ref[...].astype(jnp.float32)
    spread = jnp.mean(inputs * inputs, axis=-1, keepdims=True)
    normed = (inputs * lax.rsqrt(spread + epsilon) * gain_ref[...]).astype(jnp.bfloat16)
    q_ref[...] = jnp.dot(normed, w_ref[0], preferred_element_type=jnp.float32).astype(jnp.bfloat16)
    v_ref[...] = jnp.dot(normed, w_ref[2], preferred_element_type=jnp.float32).astype(jnp.bfloat16)
    kt_ref[...] = jnp.dot(normed, w_ref[1], preferred_element_type=jnp.float32).astype(jnp.bfloat16).T
    width = inputs.shape[-1]
    head_size = width // ENC_HEADS
    scale = head_size ** (-0.5)
    pair = 2 * NLEN
    rows_of = lax.broadcasted_iota(jnp.int32, (pair, pair), 0) // NLEN
    cols_of = lax.broadcasted_iota(jnp.int32, (pair, pair), 1) // NLEN
    same = rows_of == cols_of
    for b in range(inputs.shape[0] // pair):
        rows = pl.ds(b * pair, pair)
        for h in range(ENC_HEADS):
            cols = pl.ds(h * head_size, head_size)
            scores = jnp.dot(q_ref[rows, cols], kt_ref[cols, rows], preferred_element_type=jnp.float32) * scale
            weights = _softmax_bf16(jnp.where(same, scores, -jnp.inf))
            mix_ref[rows, cols] = jnp.dot(
                weights, v_ref[rows, cols], preferred_element_type=jnp.float32
            ).astype(jnp.bfloat16)
    output = jnp.dot(mix_ref[...], w_ref[3], preferred_element_type=jnp.float32)
    out_ref[...] = (inputs + output).astype(jnp.bfloat16)


def encode_blocks(blocks, gain, attention, group=8):
    count, length, width = blocks.shape
    group = min(group, count)
    rows = group * length
    flat = blocks.reshape(count * length, width)
    return pl.pallas_call(
        _encoder_kernel,
        out_shape=jax.ShapeDtypeStruct(flat.shape, jnp.bfloat16),
        grid=(count // group,),
        in_specs=[
            pl.BlockSpec((rows, width), lambda i: (i, 0)),
            pl.BlockSpec((1, width), lambda i: (0, 0)),
            pl.BlockSpec(attention.shape, lambda i: (0, 0, 0)),
        ],
        out_specs=pl.BlockSpec((rows, width), lambda i: (i, 0)),
        scratch_shapes=[
            pltpu.VMEM((rows, width), jnp.bfloat16),
            pltpu.VMEM((width, rows), jnp.bfloat16),
            pltpu.VMEM((rows, width), jnp.bfloat16),
            pltpu.VMEM((rows, width), jnp.bfloat16),
        ],
    )(flat, gain.reshape(1, width), attention)


def _cross_kernel(q_ref, kt_ref, enc_ref, wv_ref, out_ref, v_ref):
    v_ref[...] = jnp.dot(enc_ref[...], wv_ref[...], preferred_element_type=jnp.float32).astype(jnp.bfloat16)
    scale = HEAD_DIM ** (-0.5)
    memory = NEIGH * NLEN
    for s in range(q_ref.shape[0] // SPAN):
        rq = pl.ds(s * SPAN, SPAN)
        rk = pl.ds(s * memory, memory)
        for h in range(q_ref.shape[-1] // HEAD_DIM):
            cols = pl.ds(h * HEAD_DIM, HEAD_DIM)
            scores = jnp.dot(q_ref[rq, cols], kt_ref[cols, rk], preferred_element_type=jnp.float32) * scale
            weights = _softmax_bf16(scores)
            out_ref[rq, cols] = jnp.dot(
                weights, v_ref[rk, cols], preferred_element_type=jnp.float32
            ).astype(jnp.bfloat16)


def cross_attend(queries, keys_t, encoded, value_weight, group=4):
    length, width = queries.shape
    enc_width = encoded.shape[-1]
    memory = NEIGH * NLEN
    group = min(group, length // SPAN)
    return pl.pallas_call(
        _cross_kernel,
        out_shape=jax.ShapeDtypeStruct(queries.shape, jnp.bfloat16),
        grid=(length // (SPAN * group),),
        in_specs=[
            pl.BlockSpec((SPAN * group, width), lambda c: (c, 0)),
            pl.BlockSpec((width, memory * group), lambda c: (0, c)),
            pl.BlockSpec((memory * group, enc_width), lambda c: (c, 0)),
            pl.BlockSpec(value_weight.shape, lambda c: (0, 0)),
        ],
        out_specs=pl.BlockSpec((SPAN * group, width), lambda c: (c, 0)),
        scratch_shapes=[pltpu.VMEM((memory * group, width), jnp.bfloat16)],
    )(queries, keys_t, encoded, value_weight)


def gather_weights(shard, n_dp):
    n_x = n_dp // 2
    place = lax.axis_index("dp")
    x, core = place // 2, place % 2
    pieces = [(shard, place)]
    for shift in range(1, n_x):
        ring = [(src, ((src // 2 + shift) % n_x) * 2 + src % 2) for src in range(n_dp)]
        pieces.append((lax.ppermute(shard, "dp", ring), ((x - shift) % n_x) * 2 + core))
    swap = [(src, src ^ 1) for src in range(n_dp)]
    pieces += [(lax.ppermute(piece, "dp", swap), owner ^ 1) for piece, owner in pieces]
    count, rows, width = shard.shape
    full = jnp.zeros((count, n_dp * rows, width), shard.dtype)
    for piece, owner in pieces:
        full = lax.dynamic_update_slice(full, piece, (0, owner * rows, 0))
    return full


def make_shards(n_seq, n_dp):
    def shards(queries, neighbour_input, owner_list, block_list, enc_gain, enc_attn, kv_weight):
        full_weights = gather_weights(enc_attn, n_dp)
        me = lax.axis_index("seq")
        owners = owner_list.reshape(-1)
        indices = block_list.reshape(-1)
        refs = owners.shape[0]
        per_owner = -(-refs // n_seq)
        same = owners[:, None] == owners[None, :]
        earlier = jnp.arange(refs)[None, :] < jnp.arange(refs)[:, None]
        rank = jnp.sum(same & earlier, axis=1).astype(jnp.int32)
        asks = jnp.stack([owners, indices, rank])
        asks = jnp.broadcast_to(asks[None], (n_seq, 3, refs))
        asked = lax.all_to_all(asks, "seq", 0, 0, tiled=True)
        slots = jnp.arange(per_owner, dtype=jnp.int32)
        match = (asked[:, 0, None, :] == me) & (asked[:, 2, None, :] == slots[None, :, None])
        picks = jnp.sum(jnp.where(match, asked[:, 1, None, :], 0), axis=-1)
        sent = jnp.take(neighbour_input[0], picks.reshape(-1), axis=0, mode="clip")
        sent = sent.reshape(n_seq, per_owner, NLEN, neighbour_input.shape[-1])
        got = lax.all_to_all(sent, "seq", 0, 0, tiled=True)
        got = got.reshape(n_seq * per_owner, NLEN, neighbour_input.shape[-1])
        chosen_raw = jnp.take(got, owners * per_owner + rank, axis=0, mode="clip")
        chosen = encode_blocks(chosen_raw, enc_gain, full_weights)
        keys_t = jnp.einsum(
            "ef,re->fr", kv_weight[0], chosen, preferred_element_type=jnp.float32
        ).astype(jnp.bfloat16)
        return cross_attend(queries[0], keys_t, chosen, kv_weight[1])[None]

    return shards


def solution(mesh):
    return jax.shard_map(
        make_shards(mesh.shape["seq"], mesh.shape["dp"]),
        mesh=mesh,
        in_specs=(
            P("dp", "seq", None),
            P("dp", "seq", None, None),
            P("dp", "seq", None),
            P("dp", "seq", None),
            P(),
            P(None, "dp", None),
            P(),
        ),
        out_specs=P("dp", "seq", None),
        check_vma=False,
    )
```

```python
import jax
import jax.numpy as jnp
from jax import lax
from jax.experimental import pallas as pl
from jax.experimental.pallas import tpu as pltpu
from jax.sharding import PartitionSpec as P

HEADS = 16
HEAD_DIM = 128
ENC_HEADS = 7
NLEN = 64
SPAN = 64
NEIGH = 2
NB_DEV = 4


epsilon = 1e-05


def _softmax_bf16(scores):
    highest = jnp.max(scores, axis=-1, keepdims=True)
    raised = jnp.exp(scores - highest)
    return (raised * (1.0 / jnp.sum(raised, axis=-1, keepdims=True))).astype(jnp.bfloat16)


def _encoder_kernel(x_ref, gain_ref, w_ref, out_ref, q_ref, kt_ref, v_ref, mix_ref):
    inputs = x_ref[...].astype(jnp.float32)
    spread = jnp.mean(inputs * inputs, axis=-1, keepdims=True)
    normed = (inputs * lax.rsqrt(spread + epsilon) * gain_ref[...]).astype(jnp.bfloat16)
    q_ref[...] = jnp.dot(normed, w_ref[0], preferred_element_type=jnp.float32).astype(jnp.bfloat16)
    v_ref[...] = jnp.dot(normed, w_ref[2], preferred_element_type=jnp.float32).astype(jnp.bfloat16)
    kt_ref[...] = jnp.dot(normed, w_ref[1], preferred_element_type=jnp.float32).astype(jnp.bfloat16).T
    width = inputs.shape[-1]
    head_size = width // ENC_HEADS
    scale = head_size ** (-0.5)
    pair = 2 * NLEN
    rows_of = lax.broadcasted_iota(jnp.int32, (pair, pair), 0) // NLEN
    cols_of = lax.broadcasted_iota(jnp.int32, (pair, pair), 1) // NLEN
    same = rows_of == cols_of
    for b in range(inputs.shape[0] // pair):
        rows = pl.ds(b * pair, pair)
        for h in range(ENC_HEADS):
            cols = pl.ds(h * head_size, head_size)
            scores = jnp.dot(q_ref[rows, cols], kt_ref[cols, rows], preferred_element_type=jnp.float32) * scale
            weights = _softmax_bf16(jnp.where(same, scores, -jnp.inf))
            mix_ref[rows, cols] = jnp.dot(
                weights, v_ref[rows, cols], preferred_element_type=jnp.float32
            ).astype(jnp.bfloat16)
    output = jnp.dot(mix_ref[...], w_ref[3], preferred_element_type=jnp.float32)
    out_ref[...] = (inputs + output).astype(jnp.bfloat16)


def encode_blocks(blocks, gain, attention, group=8):
    count, length, width = blocks.shape
    group = min(group, count)
    rows = group * length
    flat = blocks.reshape(count * length, width)
    return pl.pallas_call(
        _encoder_kernel,
        out_shape=jax.ShapeDtypeStruct(flat.shape, jnp.bfloat16),
        grid=(count // group,),
        in_specs=[
            pl.BlockSpec((rows, width), lambda i: (i, 0)),
            pl.BlockSpec((1, width), lambda i: (0, 0)),
            pl.BlockSpec(attention.shape, lambda i: (0, 0, 0)),
        ],
        out_specs=pl.BlockSpec((rows, width), lambda i: (i, 0)),
        scratch_shapes=[
            pltpu.VMEM((rows, width), jnp.bfloat16),
            pltpu.VMEM((width, rows), jnp.bfloat16),
            pltpu.VMEM((rows, width), jnp.bfloat16),
            pltpu.VMEM((rows, width), jnp.bfloat16),
        ],
    )(flat, gain.reshape(1, width), attention)


def _cross_kernel(q_ref, enc_ref, wk_ref, wv_ref, out_ref, kt_ref, v_ref):
    encoded = enc_ref[...]
    kt_ref[...] = jnp.dot(encoded, wk_ref[...], preferred_element_type=jnp.float32).astype(jnp.bfloat16).T
    v_ref[...] = jnp.dot(encoded, wv_ref[...], preferred_element_type=jnp.float32).astype(jnp.bfloat16)
    scale = HEAD_DIM ** (-0.5)
    memory = NEIGH * NLEN
    for s in range(q_ref.shape[0] // SPAN):
        rq = pl.ds(s * SPAN, SPAN)
        rk = pl.ds(s * memory, memory)
        for h in range(q_ref.shape[-1] // HEAD_DIM):
            cols = pl.ds(h * HEAD_DIM, HEAD_DIM)
            scores = jnp.dot(q_ref[rq, cols], kt_ref[cols, rk], preferred_element_type=jnp.float32) * scale
            weights = _softmax_bf16(scores)
            out_ref[rq, cols] = jnp.dot(
                weights, v_ref[rk, cols], preferred_element_type=jnp.float32
            ).astype(jnp.bfloat16)


def cross_attend(queries, encoded, key_weight, value_weight, group=4):
    length, width = queries.shape
    enc_width = encoded.shape[-1]
    memory = NEIGH * NLEN
    group = min(group, length // SPAN)
    return pl.pallas_call(
        _cross_kernel,
        out_shape=jax.ShapeDtypeStruct(queries.shape, jnp.bfloat16),
        grid=(length // (SPAN * group),),
        in_specs=[
            pl.BlockSpec((SPAN * group, width), lambda c: (c, 0)),
            pl.BlockSpec((memory * group, enc_width), lambda c: (c, 0)),
            pl.BlockSpec(key_weight.shape, lambda c: (0, 0)),
            pl.BlockSpec(value_weight.shape, lambda c: (0, 0)),
        ],
        out_specs=pl.BlockSpec((SPAN * group, width), lambda c: (c, 0)),
        scratch_shapes=[
            pltpu.VMEM((width, memory * group), jnp.bfloat16),
            pltpu.VMEM((memory * group, width), jnp.bfloat16),
        ],
    )(queries, encoded, key_weight, value_weight)


def gather_weights(shard, n_dp):
    n_x = n_dp // 2
    place = lax.axis_index("dp")
    x, core = place // 2, place % 2
    pieces = [(shard, place)]
    for shift in range(1, n_x):
        ring = [(src, ((src // 2 + shift) % n_x) * 2 + src % 2) for src in range(n_dp)]
        pieces.append((lax.ppermute(shard, "dp", ring), ((x - shift) % n_x) * 2 + core))
    swap = [(src, src ^ 1) for src in range(n_dp)]
    pieces += [(lax.ppermute(piece, "dp", swap), owner ^ 1) for piece, owner in pieces]
    count, rows, width = shard.shape
    full = jnp.zeros((count, n_dp * rows, width), shard.dtype)
    for piece, owner in pieces:
        full = lax.dynamic_update_slice(full, piece, (0, owner * rows, 0))
    return full


def make_shards(n_seq, n_dp):
    def shards(queries, neighbour_input, owner_list, block_list, enc_gain, enc_attn, kv_weight):
        full_weights = gather_weights(enc_attn, n_dp)
        me = lax.axis_index("seq")
        owners = owner_list.reshape(-1)
        indices = block_list.reshape(-1)
        refs = owners.shape[0]
        per_owner = -(-refs // n_seq)
        same = owners[:, None] == owners[None, :]
        earlier = jnp.arange(refs)[None, :] < jnp.arange(refs)[:, None]
        rank = jnp.sum(same & earlier, axis=1).astype(jnp.int32)
        asks = jnp.stack([owners, indices, rank])
        asks = jnp.broadcast_to(asks[None], (n_seq, 3, refs))
        asked = lax.all_to_all(asks, "seq", 0, 0, tiled=True)
        slots = jnp.arange(per_owner, dtype=jnp.int32)
        match = (asked[:, 0, None, :] == me) & (asked[:, 2, None, :] == slots[None, :, None])
        picks = jnp.sum(jnp.where(match, asked[:, 1, None, :], 0), axis=-1)
        sent = jnp.take(neighbour_input[0], picks.reshape(-1), axis=0, mode="clip")
        sent = sent.reshape(n_seq, per_owner, NLEN, neighbour_input.shape[-1])
        got = lax.all_to_all(sent, "seq", 0, 0, tiled=True)
        got = got.reshape(n_seq * per_owner, NLEN, neighbour_input.shape[-1])
        chosen_raw = jnp.take(got, owners * per_owner + rank, axis=0, mode="clip")
        chosen = encode_blocks(chosen_raw, enc_gain, full_weights)
        return cross_attend(queries[0], chosen, kv_weight[0], kv_weight[1])[None]

    return shards


def solution(mesh):
    return jax.shard_map(
        make_shards(mesh.shape["seq"], mesh.shape["dp"]),
        mesh=mesh,
        in_specs=(
            P("dp", "seq", None),
            P("dp", "seq", None, None),
            P("dp", "seq", None),
            P("dp", "seq", None),
            P(),
            P(None, "dp", None),
            P(),
        ),
        out_specs=P("dp", "seq", None),
        check_vma=False,
    )
```

```python
import jax
import jax.numpy as jnp
from jax import lax
from jax.experimental import pallas as pl
from jax.experimental.pallas import tpu as pltpu
from jax.sharding import PartitionSpec as P

HEADS = 16
HEAD_DIM = 128
ENC_HEADS = 7
NLEN = 64
SPAN = 64
NEIGH = 2
NB_DEV = 4


epsilon = 1e-05


def _softmax_bf16(scores):
    highest = jnp.max(scores, axis=-1, keepdims=True)
    raised = jnp.exp(scores - highest)
    return (raised * (1.0 / jnp.sum(raised, axis=-1, keepdims=True))).astype(jnp.bfloat16)


def _encoder_kernel(x_ref, gain_ref, w_ref, out_ref, q_ref, kt_ref, v_ref, mix_ref):
    inputs = x_ref[...].astype(jnp.float32)
    spread = jnp.mean(inputs * inputs, axis=-1, keepdims=True)
    normed = (inputs * lax.rsqrt(spread + epsilon) * gain_ref[...]).astype(jnp.bfloat16)
    q_ref[...] = jnp.dot(normed, w_ref[0], preferred_element_type=jnp.float32).astype(jnp.bfloat16)
    v_ref[...] = jnp.dot(normed, w_ref[2], preferred_element_type=jnp.float32).astype(jnp.bfloat16)
    kt_ref[...] = jnp.dot(normed, w_ref[1], preferred_element_type=jnp.float32).astype(jnp.bfloat16).T
    width = inputs.shape[-1]
    head_size = width // ENC_HEADS
    scale = head_size ** (-0.5)
    pair = 2 * NLEN
    rows_of = lax.broadcasted_iota(jnp.int32, (pair, pair), 0) // NLEN
    cols_of = lax.broadcasted_iota(jnp.int32, (pair, pair), 1) // NLEN
    same = rows_of == cols_of
    for b in range(inputs.shape[0] // pair):
        rows = pl.ds(b * pair, pair)
        for h in range(ENC_HEADS):
            cols = pl.ds(h * head_size, head_size)
            scores = jnp.dot(q_ref[rows, cols], kt_ref[cols, rows], preferred_element_type=jnp.float32) * scale
            weights = _softmax_bf16(jnp.where(same, scores, -jnp.inf))
            mix_ref[rows, cols] = jnp.dot(
                weights, v_ref[rows, cols], preferred_element_type=jnp.float32
            ).astype(jnp.bfloat16)
    output = jnp.dot(mix_ref[...], w_ref[3], preferred_element_type=jnp.float32)
    out_ref[...] = (inputs + output).astype(jnp.bfloat16)


def encode_blocks(blocks, gain, attention, group=8):
    count, length, width = blocks.shape
    group = min(group, count)
    rows = group * length
    flat = blocks.reshape(count * length, width)
    return pl.pallas_call(
        _encoder_kernel,
        out_shape=jax.ShapeDtypeStruct(flat.shape, jnp.bfloat16),
        grid=(count // group,),
        in_specs=[
            pl.BlockSpec((rows, width), lambda i: (i, 0)),
            pl.BlockSpec((1, width), lambda i: (0, 0)),
            pl.BlockSpec(attention.shape, lambda i: (0, 0, 0)),
        ],
        out_specs=pl.BlockSpec((rows, width), lambda i: (i, 0)),
        scratch_shapes=[
            pltpu.VMEM((rows, width), jnp.bfloat16),
            pltpu.VMEM((width, rows), jnp.bfloat16),
            pltpu.VMEM((rows, width), jnp.bfloat16),
            pltpu.VMEM((rows, width), jnp.bfloat16),
        ],
    )(flat, gain.reshape(1, width), attention)


def _cross_kernel(q_ref, enc_ref, wk_ref, wv_ref, out_ref, kt_ref, v_ref):
    encoded = enc_ref[...]
    kt_ref[...] = jnp.dot(encoded, wk_ref[...], preferred_element_type=jnp.float32).astype(jnp.bfloat16).T
    v_ref[...] = jnp.dot(encoded, wv_ref[...], preferred_element_type=jnp.float32).astype(jnp.bfloat16)
    scale = HEAD_DIM ** (-0.5)
    memory = NEIGH * NLEN
    for s in range(q_ref.shape[0] // SPAN):
        rq = pl.ds(s * SPAN, SPAN)
        rk = pl.ds(s * memory, memory)
        for h in range(q_ref.shape[-1] // HEAD_DIM):
            cols = pl.ds(h * HEAD_DIM, HEAD_DIM)
            scores = jnp.dot(q_ref[rq, cols], kt_ref[cols, rk], preferred_element_type=jnp.float32) * scale
            weights = _softmax_bf16(scores)
            out_ref[rq, cols] = jnp.dot(
                weights, v_ref[rk, cols], preferred_element_type=jnp.float32
            ).astype(jnp.bfloat16)


def cross_attend(queries, encoded, key_weight, value_weight, group=2):
    length, width = queries.shape
    enc_width = encoded.shape[-1]
    memory = NEIGH * NLEN
    group = min(group, length // SPAN)
    return pl.pallas_call(
        _cross_kernel,
        out_shape=jax.ShapeDtypeStruct(queries.shape, jnp.bfloat16),
        grid=(length // (SPAN * group),),
        in_specs=[
            pl.BlockSpec((SPAN * group, width), lambda c: (c, 0)),
            pl.BlockSpec((memory * group, enc_width), lambda c: (c, 0)),
            pl.BlockSpec(key_weight.shape, lambda c: (0, 0)),
            pl.BlockSpec(value_weight.shape, lambda c: (0, 0)),
        ],
        out_specs=pl.BlockSpec((SPAN * group, width), lambda c: (c, 0)),
        scratch_shapes=[
            pltpu.VMEM((width, memory * group), jnp.bfloat16),
            pltpu.VMEM((memory * group, width), jnp.bfloat16),
        ],
    )(queries, encoded, key_weight, value_weight)


def gather_weights(shard, n_dp):
    n_x = n_dp // 2
    place = lax.axis_index("dp")
    x, core = place // 2, place % 2
    pieces = [(shard, place)]
    for shift in range(1, n_x):
        ring = [(src, ((src // 2 + shift) % n_x) * 2 + src % 2) for src in range(n_dp)]
        pieces.append((lax.ppermute(shard, "dp", ring), ((x - shift) % n_x) * 2 + core))
    swap = [(src, src ^ 1) for src in range(n_dp)]
    pieces += [(lax.ppermute(piece, "dp", swap), owner ^ 1) for piece, owner in pieces]
    count, rows, width = shard.shape
    full = jnp.zeros((count, n_dp * rows, width), shard.dtype)
    for piece, owner in pieces:
        full = lax.dynamic_update_slice(full, piece, (0, owner * rows, 0))
    return full


def make_shards(n_seq, n_dp):
    def shards(queries, neighbour_input, owner_list, block_list, enc_gain, enc_attn, kv_weight):
        full_weights = gather_weights(enc_attn, n_dp)
        me = lax.axis_index("seq")
        owners = owner_list.reshape(-1)
        indices = block_list.reshape(-1)
        refs = owners.shape[0]
        per_owner = -(-refs // n_seq)
        same = owners[:, None] == owners[None, :]
        earlier = jnp.arange(refs)[None, :] < jnp.arange(refs)[:, None]
        rank = jnp.sum(same & earlier, axis=1).astype(jnp.int32)
        asks = jnp.stack([owners, indices, rank])
        asks = jnp.broadcast_to(asks[None], (n_seq, 3, refs))
        asked = lax.all_to_all(asks, "seq", 0, 0, tiled=True)
        slots = jnp.arange(per_owner, dtype=jnp.int32)
        match = (asked[:, 0, None, :] == me) & (asked[:, 2, None, :] == slots[None, :, None])
        picks = jnp.sum(jnp.where(match, asked[:, 1, None, :], 0), axis=-1)
        sent = jnp.take(neighbour_input[0], picks.reshape(-1), axis=0, mode="clip")
        sent = sent.reshape(n_seq, per_owner, NLEN, neighbour_input.shape[-1])
        got = lax.all_to_all(sent, "seq", 0, 0, tiled=True)
        got = got.reshape(n_seq * per_owner, NLEN, neighbour_input.shape[-1])
        chosen_raw = jnp.take(got, owners * per_owner + rank, axis=0, mode="clip")
        chosen = encode_blocks(chosen_raw, enc_gain, full_weights)
        return cross_attend(queries[0], chosen, kv_weight[0], kv_weight[1])[None]

    return shards


def solution(mesh):
    return jax.shard_map(
        make_shards(mesh.shape["seq"], mesh.shape["dp"]),
        mesh=mesh,
        in_specs=(
            P("dp", "seq", None),
            P("dp", "seq", None, None),
            P("dp", "seq", None),
            P("dp", "seq", None),
            P(),
            P(None, "dp", None),
            P(),
        ),
        out_specs=P("dp", "seq", None),
        check_vma=False,
    )
```
